32 devices in a mesh: grp: 2 (over y), row: 4 (over z), col: 2 (over x), sub: 2 (over core).
Axes of the slice: x: 2, y: 2, z: 4, core: 2. Of those that a mesh axis runs over, the one named last changes fastest.
Arguments:
- a_blocks: bfloat16 [16, 2, 4, 2, 256, 256], P(('grp', 'row', 'sub'), 'col'), parts along dimension 0, may hold values from 20 to 2000
- block_list: int32 [16, 2, 4, 2], P(('grp', 'row', 'sub'), 'col'), parts along dimension 0, may hold values from 0 to 3, as said below
- block_count: int32 [16, 2, 4], P(('grp', 'row', 'sub'), 'col'), parts along dimension 0, may hold values from 1 to 2
- w_factor: bfloat16 [16, 1024, 256], P(('grp', 'row', 'sub')), parts along dimension 0, may hold values from 0.05 to 4
- h_factor: bfloat16 [256, 4096], P(None, ('grp', 'row', 'col')), parts along dimension 1, may hold values from 0.05 to 4
Outputs:
- w_new: float32 [16, 1024, 256], P(('grp', 'row', 'sub'), 'col'), parts along dimension 0
- h_new: float32 [256, 4096], P(None, ('grp', 'row', 'col')), parts along dimension 1
The draws below stay inside these ranges and needn't reach their ends.
There are 2 independent parts, one for each index of `grp`. The reference program is written for one: setup_inputs(seed, part) draws one part's arguments, and reference() takes and returns one part's arrays. A program takes and returns all parts, laid end to end along the dimension named above; each array names one. Nothing has to cross between parts.
Inputs may be any that keep to these rules, and one draw needn't show every extreme that they name: `block_list`: within one block row and column group the 2 slots name different column blocks.
All inputs are finite; a program needn't handle non-finite values.
Results may differ from the reference program's by a relative error of at most 0.0003.
Values may be sent and summed in bfloat16 or wider, within the bound.
No kernel may reach another device: no remote copies, remote signals or barrier semaphores. Data moves between devices by JAX's collectives and lax.ppermute only.
A program may use at most 64 MiB of HBM per device.

```python
import math
import jax
import jax.numpy as jnp
from jax import lax

RANK = 256
BLOCK = 256
ROW_BLOCKS = 4
SLOTS = 2
TILES = 8
TILE_ROWS = 1024
COLUMNS = 2048
N_ROW = 4
N_COL = 2


def draw_block_list(key, part):
    total = TILES * N_COL * ROW_BLOCKS
    keys = jax.random.split(jax.random.fold_in(key, 11), total)
    chosen = jax.vmap(lambda k: jax.random.permutation(k, N_ROW)[:SLOTS])(keys)
    return chosen.reshape(TILES, N_COL, ROW_BLOCKS, SLOTS).astype(jnp.int32)


def draw_block_count(key, part):
    total = TILES * N_COL * ROW_BLOCKS
    first = jax.random.randint(jax.random.fold_in(key, 21), (total,), 1, SLOTS + 1)
    second = jax.random.randint(jax.random.fold_in(key, 22), (total,), 1, SLOTS + 1)
    counts = jnp.minimum(first, second)
    pick = jax.random.randint(jax.random.fold_in(key, 23), (), 0, total)
    counts = jnp.where(jnp.arange(total) == pick, SLOTS, counts)
    return counts.reshape(TILES, N_COL, ROW_BLOCKS).astype(jnp.int32)


def draw_w_factor(key, part):
    shape = (TILES, TILE_ROWS, RANK)
    position = jnp.arange(TILES, dtype=jnp.float32)[:, None, None] / max(TILES - 1, 1)
    base = jnp.exp(jax.random.uniform(jax.random.fold_in(key, 32), shape, jnp.float32, jnp.log(0.1), 0.0))
    factor = jnp.power(3.0, position)
    return (base * factor).astype(jnp.bfloat16)


def draw_h_factor(key, part):
    shape = (RANK, COLUMNS)
    blocks = N_ROW * N_COL
    position = (jnp.arange(COLUMNS, dtype=jnp.int32) // BLOCK).astype(jnp.float32)[None, :] / max(blocks - 1, 1)
    base = jnp.exp(jax.random.uniform(jax.random.fold_in(key, 42), shape, jnp.float32, jnp.log(0.1), 0.0))
    factor = jnp.power(3.0, position)
    return (base * factor).astype(jnp.bfloat16)


def block_scale(rng, shape, cuts, low, largest):
    factor_of = 1.0
    for dim, shards_of in cuts:
        draws = jax.random.uniform(jax.random.fold_in(jax.random.fold_in(rng, 6), dim), (shards_of,), jnp.float32, low / len(cuts), largest / len(cuts))
        factor_of = factor_of * jnp.repeat(jnp.exp(draws), shape[dim] // shards_of).reshape((-1,) + (1,) * (len(shape) - 1 - dim))
    return factor_of


def setup_inputs(seed: int = 0, part: int = 0) -> dict:
    key_list = jax.random.split(jax.random.key(seed), 6)
    part_keys = jax.random.split(jax.random.fold_in(key_list[5], part), 6)
    a_blocks = jnp.clip(jnp.exp(math.log(2000.0) - 4.6051702 * jax.random.uniform(part_keys[0], (TILES, N_COL, ROW_BLOCKS, SLOTS, BLOCK, BLOCK), jnp.float32) ** block_scale(part_keys[0], (TILES, N_COL, ROW_BLOCKS, SLOTS, BLOCK, BLOCK), ((0, 8), (1, 2)), -0.2, 0.2)), 20.0, 2000.0).astype(jnp.bfloat16)
    block_list = draw_block_list(jax.random.fold_in(jax.random.fold_in(key_list[5], part), 71), part)
    block_count = draw_block_count(jax.random.fold_in(jax.random.fold_in(key_list[5], part), 71), part)
    w_factor = draw_w_factor(jax.random.fold_in(jax.random.fold_in(key_list[5], part), 71), part)
    h_factor = draw_h_factor(jax.random.fold_in(jax.random.fold_in(key_list[5], part), 71), part)
    return dict(a_blocks=a_blocks, block_list=block_list, block_count=block_count, w_factor=w_factor, h_factor=h_factor)


def reference(a_blocks, block_list, block_count, w_factor, h_factor):
    w_total = jnp.sum(w_factor.astype(jnp.float32), axis=(0, 1))
    h_total = jnp.sum(h_factor.astype(jnp.float32), axis=1)
    total_slots = TILES * N_COL * ROW_BLOCKS * SLOTS
    numer_w = jnp.zeros((TILES, TILE_ROWS, RANK), jnp.float32)
    numer_h = jnp.zeros((RANK, COLUMNS), jnp.float32)

    def visit(state, index):
        slot_idx = index % SLOTS
        rest = index // SLOTS
        brow = rest % ROW_BLOCKS
        rest = rest // ROW_BLOCKS
        group = rest % N_COL
        tile = (rest // N_COL).astype(jnp.int32)
        matches = slot_idx < block_count[tile, group, brow]
        column = (block_list[tile, group, brow, slot_idx] * N_COL + group).astype(jnp.int32)
        row_start = (brow * BLOCK).astype(jnp.int32)
        col_start = (column * BLOCK).astype(jnp.int32)
        zero = jnp.int32(0)

        def compute(state):
            numer_w, numer_h = state
            w_rows = lax.dynamic_slice(w_factor, (tile, row_start, zero), (1, BLOCK, RANK))[0]
            h_block = lax.dynamic_slice(h_factor, (zero, col_start), (RANK, BLOCK))
            values = a_blocks[tile, group, brow, slot_idx]
            product = jnp.dot(w_rows, h_block, preferred_element_type=jnp.float32)
            ratios = (values.astype(jnp.float32) / product).astype(jnp.bfloat16)
            part_h = jnp.dot(w_rows.T, ratios, preferred_element_type=jnp.float32)
            part_w = jnp.dot(ratios, h_block.T, preferred_element_type=jnp.float32)
            old_h = lax.dynamic_slice(numer_h, (zero, col_start), (RANK, BLOCK))
            numer_h = lax.dynamic_update_slice(numer_h, old_h + part_h, (zero, col_start))
            old_w = lax.dynamic_slice(numer_w, (tile, row_start, zero), (1, BLOCK, RANK))
            numer_w = lax.dynamic_update_slice(numer_w, old_w + part_w[None], (tile, row_start, zero))
            return numer_w, numer_h

        return lax.cond(matches, compute, lambda st: st, state), None

    (numer_w, numer_h), _ = lax.scan(visit, (numer_w, numer_h), jnp.arange(total_slots, dtype=jnp.int32))
    w_new = w_factor.astype(jnp.float32) * numer_w / h_total[None, None, :]
    h_new = h_factor.astype(jnp.float32) * numer_h / w_total[:, None]
    return w_new, h_new
```

```python
import jax
import jax.numpy as jnp
from jax import lax
from jax.sharding import PartitionSpec as P


def body(a_blocks, block_list, block_count, w_factor, h_factor):
    values = a_blocks[0, 0]
    lists = block_list[0, 0]
    counts = block_count[0, 0]
    w_tile = w_factor[0]
    row_blocks, stored, width = values.shape[0], values.shape[1], values.shape[2]
    rank = w_tile.shape[1]
    tile_rows = w_tile.shape[0]
    n_row = lax.axis_size("row")
    w_rows = w_tile.reshape(row_blocks, width, rank)

    h_all = lax.all_gather(h_factor, "row", axis=1, tiled=True)

    numer_h = jnp.zeros((rank, n_row * width), jnp.float32)
    parts_w = []
    for brow in range(row_blocks):
        part_w = jnp.zeros((width, rank), jnp.float32)
        for slot in range(stored):
            target = lists[brow, slot]
            live = slot < counts[brow]
            h_block = lax.dynamic_slice_in_dim(h_all, target * width, width, 1)
            product = jnp.dot(w_rows[brow], h_block, preferred_element_type=jnp.float32)
            ratios = (values[brow, slot].astype(jnp.float32) / product).astype(jnp.bfloat16)
            ratios = jnp.where(live, ratios, jnp.zeros_like(ratios))
            part_h = jnp.einsum(
                "ik,ij->kj", w_rows[brow], ratios, preferred_element_type=jnp.float32
            )
            part_w = part_w + jnp.einsum(
                "ij,kj->ik", ratios, h_block, preferred_element_type=jnp.float32
            )
            old = lax.dynamic_slice_in_dim(numer_h, target * width, width, 1)
            numer_h = lax.dynamic_update_slice_in_dim(numer_h, old + part_h, target * width, 1)
        parts_w.append(part_w)
    numer_w = jnp.stack(parts_w).reshape(tile_rows, rank)

    col_first = lax.axis_index("col") == 0
    sub_first = lax.axis_index("sub") == 0
    w_sum = jnp.sum(w_tile.astype(jnp.float32), axis=0)
    h_sum = jnp.sum(h_factor.astype(jnp.float32), axis=1)
    sums = jnp.concatenate(
        [jnp.where(col_first, w_sum, 0.0), jnp.where(sub_first, h_sum, 0.0)]
    )
    sums = lax.psum(sums, ("row", "col", "sub"))
    w_total = sums[:rank]
    h_total = sums[rank:]

    numer_h = lax.psum_scatter(numer_h, "row", scatter_dimension=1, tiled=True)
    numer_h = lax.psum(numer_h, "sub")
    h_new = h_factor.astype(jnp.float32) * numer_h / w_total[:, None]

    share = tile_rows // lax.axis_size("col")
    col_index = lax.axis_index("col")
    mine = lax.psum_scatter(numer_w, "col", scatter_dimension=0, tiled=True)
    w_part = lax.dynamic_slice_in_dim(w_tile, col_index * share, share, 0).astype(jnp.float32)
    w_new = (w_part * mine / h_total[None, :])[None]
    return (w_new, h_new)


def solution(mesh):
    placed = (
        P(("grp", "row", "sub"), "col", None, None, None, None),
        P(("grp", "row", "sub"), "col", None, None),
        P(("grp", "row", "sub"), "col", None),
        P(("grp", "row", "sub"), None, None),
        P(None, ("grp", "row", "col")),
    )
    return jax.shard_map(
        body,
        mesh=mesh,
        in_specs=placed,
        out_specs=(P(("grp", "row", "sub"), "col", None), P(None, ("grp", "row", "col"))),
        check_vma=False,
    )
```

```python
import jax
import jax.numpy as jnp
from jax import lax
from jax.sharding import PartitionSpec as P


def shifted(value, axis, by):
    length = lax.axis_size(axis)
    return lax.ppermute(value, axis, [(i, (i + by) % length) for i in range(length)])


def as_rows(vector, width):
    size = vector.shape[0]
    rows = -(-size // width)
    flat = jnp.pad(vector, (0, rows * width - size)).reshape(rows, width)
    return jnp.pad(flat, ((0, (-rows) % 8), (0, 0)))


def from_rows(rows, size):
    return rows.reshape(-1)[:size]


def body(a_blocks, block_list, block_count, w_factor, h_factor):
    values = a_blocks[0, 0]
    lists = block_list[0, 0]
    counts = block_count[0, 0]
    w_tile = w_factor[0]
    row_blocks, stored, width = values.shape[0], values.shape[1], values.shape[2]
    rank = w_tile.shape[1]
    tile_rows = w_tile.shape[0]
    n_row = lax.axis_size("row")
    n_col = lax.axis_size("col")
    n_sub = lax.axis_size("sub")
    row_index = lax.axis_index("row")
    col_index = lax.axis_index("col")
    w_rows = w_tile.reshape(row_blocks, width, rank)

    h_stack = jnp.stack([h_factor] + [shifted(h_factor, "row", d) for d in range(1, n_row)])
    h_sum = jnp.sum(h_stack.astype(jnp.float32), axis=(0, 2))
    w_sum = jnp.sum(w_tile.astype(jnp.float32), axis=0)

    numer_h_stack = jnp.zeros((n_row, rank, width), jnp.float32)
    parts_w = []
    for brow in range(row_blocks):
        part_w = jnp.zeros((width, rank), jnp.float32)
        for slot in range(stored):
            target = lists[brow, slot]
            live = slot < counts[brow]
            h_block = lax.dynamic_index_in_dim(
                h_stack, (row_index - target) % n_row, 0, keepdims=False
            )
            product = jnp.dot(w_rows[brow], h_block, preferred_element_type=jnp.float32)
            ratios = (values[brow, slot].astype(jnp.float32) / product).astype(jnp.bfloat16)
            ratios = jnp.where(live, ratios, jnp.zeros_like(ratios))
            part_h = jnp.einsum(
                "ik,ij->kj", w_rows[brow], ratios, preferred_element_type=jnp.float32
            )
            part_w = part_w + jnp.einsum(
                "ij,kj->ik", ratios, h_block, preferred_element_type=jnp.float32
            )
            offset = (target - row_index) % n_row
            old = lax.dynamic_index_in_dim(numer_h_stack, offset, 0, keepdims=True)
            numer_h_stack = lax.dynamic_update_index_in_dim(
                numer_h_stack, old + part_h[None], offset, 0
            )
        parts_w.append(part_w)
    numer_w = jnp.stack(parts_w).reshape(tile_rows, rank)

    share = tile_rows // n_col
    chunks = numer_w.reshape(n_col, share, rank)
    h_rows = as_rows(h_sum, rank)
    mine_w = lax.dynamic_index_in_dim(chunks, col_index, 0, keepdims=False)
    got_h = h_rows
    for d in range(1, n_col):
        chunk = lax.dynamic_index_in_dim(chunks, (col_index + d) % n_col, 0, keepdims=False)
        message = shifted(jnp.concatenate([chunk, h_rows]), "col", d)
        mine_w = mine_w + message[:share]
        got_h = got_h + message[share:]
    h_total = from_rows(got_h, rank)

    w_rows_sum = as_rows(w_sum, width)
    mine_h = numer_h_stack[0]
    got_w = w_rows_sum
    for d in range(1, n_row):
        message = shifted(jnp.concatenate([numer_h_stack[d], w_rows_sum]), "row", d)
        mine_h = mine_h + message[:rank]
        got_w = got_w + message[rank:]
    both = jnp.concatenate([mine_h, got_w])
    total = both
    for d in range(1, n_sub):
        total = total + shifted(both, "sub", d)
    numer_h = total[:rank]
    w_total = from_rows(total[rank:], rank)

    h_new = h_factor.astype(jnp.float32) * numer_h / w_total[:, None]
    w_part = lax.dynamic_slice_in_dim(w_tile, col_index * share, share, 0).astype(jnp.float32)
    w_new = (w_part * mine_w / h_total[None, :])[None]
    return (w_new, h_new)


def solution(mesh):
    placed = (
        P(("grp", "row", "sub"), "col", None, None, None, None),
        P(("grp", "row", "sub"), "col", None, None),
        P(("grp", "row", "sub"), "col", None),
        P(("grp", "row", "sub"), None, None),
        P(None, ("grp", "row", "col")),
    )
    return jax.shard_map(
        body,
        mesh=mesh,
        in_specs=placed,
        out_specs=(P(("grp", "row", "sub"), "col", None), P(None, ("grp", "row", "col"))),
        check_vma=False,
    )
```

```python
import jax
import jax.numpy as jnp
from jax import lax
from jax.sharding import PartitionSpec as P


def shifted(value, axis, by):
    length = lax.axis_size(axis)
    return lax.ppermute(value, axis, [(i, (i + by) % length) for i in range(length)])


def as_rows(vector, width):
    size = vector.shape[0]
    rows = -(-size // width)
    flat = jnp.pad(vector, (0, rows * width - size)).reshape(rows, width)
    return jnp.pad(flat, ((0, (-rows) % 8), (0, 0)))


def from_rows(rows, size):
    return rows.reshape(-1)[:size]


def dense_terms(values, lists, counts, w_tile, h_stack, row_index):
    row_blocks, stored, width = values.shape[0], values.shape[1], values.shape[2]
    n_row, rank = h_stack.shape[0], h_stack.shape[1]
    tile_rows = w_tile.shape[0]
    h_all = jnp.concatenate([h_stack[d] for d in range(n_row)], axis=1)
    block_of = (row_index - lax.iota(jnp.int32, n_row)) % n_row
    live = lax.iota(jnp.int32, stored)[None, :] < counts[:, None]
    mask = (lists[:, :, None] == block_of[None, None, :]) & live[:, :, None]
    a_dense = jnp.zeros((row_blocks, width, n_row, width), values.dtype)
    for slot in range(stored):
        a_dense = jnp.where(
            mask[:, slot, None, :, None], values[:, slot, :, None, :], a_dense
        )
    covered = jnp.any(mask, axis=1)[:, None, :, None]
    product = jnp.dot(w_tile, h_all, preferred_element_type=jnp.float32)
    product = product.reshape(row_blocks, width, n_row, width)
    ratios = jnp.where(covered, a_dense.astype(jnp.float32) / product, 0.0).astype(jnp.bfloat16)
    ratios = ratios.reshape(tile_rows, n_row * width)
    numer_h_all = jnp.einsum("ik,ij->kj", w_tile, ratios, preferred_element_type=jnp.float32)
    numer_w = jnp.einsum("ij,kj->ik", ratios, h_all, preferred_element_type=jnp.float32)
    numer_h_chunks = numer_h_all.reshape(rank, n_row, width)
    return [numer_h_chunks[:, (-e) % n_row] for e in range(n_row)], numer_w


def slot_terms(values, lists, counts, w_tile, h_stack, row_index):
    row_blocks, stored, width = values.shape[0], values.shape[1], values.shape[2]
    n_row, rank = h_stack.shape[0], h_stack.shape[1]
    tile_rows = w_tile.shape[0]
    w_rows = w_tile.reshape(row_blocks, width, rank)
    numer_h_stack = jnp.zeros((n_row, rank, width), jnp.float32)
    parts_w = []
    for brow in range(row_blocks):
        part_w = jnp.zeros((width, rank), jnp.float32)
        for slot in range(stored):
            target = lists[brow, slot]
            live = slot < counts[brow]
            h_block = lax.dynamic_index_in_dim(
                h_stack, (row_index - target) % n_row, 0, keepdims=False
            )
            product = jnp.dot(w_rows[brow], h_block, preferred_element_type=jnp.float32)
            ratios = (values[brow, slot].astype(jnp.float32) / product).astype(jnp.bfloat16)
            ratios = jnp.where(live, ratios, jnp.zeros_like(ratios))
            part_h = jnp.einsum(
                "ik,ij->kj", w_rows[brow], ratios, preferred_element_type=jnp.float32
            )
            part_w = part_w + jnp.einsum(
                "ij,kj->ik", ratios, h_block, preferred_element_type=jnp.float32
            )
            offset = (target - row_index) % n_row
            old = lax.dynamic_index_in_dim(numer_h_stack, offset, 0, keepdims=True)
            numer_h_stack = lax.dynamic_update_index_in_dim(
                numer_h_stack, old + part_h[None], offset, 0
            )
        parts_w.append(part_w)
    numer_w = jnp.stack(parts_w).reshape(tile_rows, rank)
    return [numer_h_stack[e] for e in range(n_row)], numer_w


def body(a_blocks, block_list, block_count, w_factor, h_factor):
    values = a_blocks[0, 0]
    lists = block_list[0, 0]
    counts = block_count[0, 0]
    w_tile = w_factor[0]
    row_blocks, stored, width = values.shape[0], values.shape[1], values.shape[2]
    rank = w_tile.shape[1]
    tile_rows = w_tile.shape[0]
    n_row = lax.axis_size("row")
    n_col = lax.axis_size("col")
    n_sub = lax.axis_size("sub")
    row_index = lax.axis_index("row")
    col_index = lax.axis_index("col")

    h_stack = jnp.stack([h_factor] + [shifted(h_factor, "row", d) for d in range(1, n_row)])
    h_sum = jnp.sum(h_stack.astype(jnp.float32), axis=(0, 2))
    w_sum = jnp.sum(w_tile.astype(jnp.float32), axis=0)

    if tile_rows * n_row * width * 4 <= (8 << 20):
        numer_h_stack, numer_w = dense_terms(values, lists, counts, w_tile, h_stack, row_index)
    else:
        numer_h_stack, numer_w = slot_terms(values, lists, counts, w_tile, h_stack, row_index)

    share = tile_rows // n_col
    chunks = numer_w.reshape(n_col, share, rank)
    h_rows = as_rows(h_sum, rank)
    mine_w = lax.dynamic_index_in_dim(chunks, col_index, 0, keepdims=False)
    got_h = h_rows
    for d in range(1, n_col):
        chunk = lax.dynamic_index_in_dim(chunks, (col_index + d) % n_col, 0, keepdims=False)
        message = shifted(jnp.concatenate([chunk, h_rows]), "col", d)
        mine_w = mine_w + message[:share]
        got_h = got_h + message[share:]
    h_total = from_rows(got_h, rank)

    w_rows_sum = as_rows(w_sum, width)
    mine_h = numer_h_stack[0]
    got_w = w_rows_sum
    for d in range(1, n_row):
        message = shifted(jnp.concatenate([numer_h_stack[d], w_rows_sum]), "row", d)
        mine_h = mine_h + message[:rank]
        got_w = got_w + message[rank:]
    both = jnp.concatenate([mine_h, got_w])
    total = both
    for d in range(1, n_sub):
        total = total + shifted(both, "sub", d)
    numer_h = total[:rank]
    w_total = from_rows(total[rank:], rank)

    h_new = h_factor.astype(jnp.float32) * numer_h / w_total[:, None]
    w_part = lax.dynamic_slice_in_dim(w_tile, col_index * share, share, 0).astype(jnp.float32)
    w_new = (w_part * mine_w / h_total[None, :])[None]
    return (w_new, h_new)


def solution(mesh):
    placed = (
        P(("grp", "row", "sub"), "col", None, None, None, None),
        P(("grp", "row", "sub"), "col", None, None),
        P(("grp", "row", "sub"), "col", None),
        P(("grp", "row", "sub"), None, None),
        P(None, ("grp", "row", "col")),
    )
    return jax.shard_map(
        body,
        mesh=mesh,
        in_specs=placed,
        out_specs=(P(("grp", "row", "sub"), "col", None), P(None, ("grp", "row", "col"))),
        check_vma=False,
    )
```

```python
import jax
import jax.numpy as jnp
from jax import lax
from jax.sharding import PartitionSpec as P


def shifted(value, axis, by):
    length = lax.axis_size(axis)
    return lax.ppermute(value, axis, [(i, (i + by) % length) for i in range(length)])


def as_rows(vector, width):
    size = vector.shape[0]
    rows = -(-size // width)
    flat = jnp.pad(vector, (0, rows * width - size)).reshape(rows, width)
    return jnp.pad(flat, ((0, (-rows) % 8), (0, 0)))


def from_rows(rows, size):
    return rows.reshape(-1)[:size]


def dense_terms(values, lists, counts, w_tile, h_stack, row_index):
    row_blocks, stored, width = values.shape[0], values.shape[1], values.shape[2]
    n_row, rank = h_stack.shape[0], h_stack.shape[1]
    tile_rows = w_tile.shape[0]
    h_all = jnp.concatenate([h_stack[d] for d in range(n_row)], axis=1)
    product = jnp.dot(w_tile, h_all, preferred_element_type=jnp.float32)
    chunks = []
    for d in range(n_row):
        block = (row_index - d) % n_row
        a_d = jnp.zeros((row_blocks, width, width), values.dtype)
        covered = jnp.zeros((row_blocks,), jnp.bool_)
        for slot in range(stored):
            match = (lists[:, slot] == block) & (slot < counts)
            a_d = jnp.where(match[:, None, None], values[:, slot], a_d)
            covered = covered | match
        p_d = product[:, d * width:(d + 1) * width].reshape(row_blocks, width, width)
        r_d = jnp.where(covered[:, None, None], a_d.astype(jnp.float32) / p_d, 0.0)
        chunks.append(r_d.astype(jnp.bfloat16).reshape(tile_rows, width))
    ratios = jnp.concatenate(chunks, axis=1)
    numer_h_all = jnp.einsum("ik,ij->kj", w_tile, ratios, preferred_element_type=jnp.float32)
    numer_w = jnp.einsum("ij,kj->ik", ratios, h_all, preferred_element_type=jnp.float32)
    starts = [((-e) % n_row) * width for e in range(n_row)]
    return [numer_h_all[:, s:s + width] for s in starts], numer_w


def slot_terms(values, lists, counts, w_tile, h_stack, row_index):
    row_blocks, stored, width = values.shape[0], values.shape[1], values.shape[2]
    n_row, rank = h_stack.shape[0], h_stack.shape[1]
    tile_rows = w_tile.shape[0]
    w_rows = w_tile.reshape(row_blocks, width, rank)
    numer_h_stack = jnp.zeros((n_row, rank, width), jnp.float32)
    parts_w = []
    for brow in range(row_blocks):
        part_w = jnp.zeros((width, rank), jnp.float32)
        for slot in range(stored):
            target = lists[brow, slot]
            live = slot < counts[brow]
            h_block = lax.dynamic_index_in_dim(
                h_stack, (row_index - target) % n_row, 0, keepdims=False
            )
            product = jnp.dot(w_rows[brow], h_block, preferred_element_type=jnp.float32)
            ratios = (values[brow, slot].astype(jnp.float32) / product).astype(jnp.bfloat16)
            ratios = jnp.where(live, ratios, jnp.zeros_like(ratios))
            part_h = jnp.einsum(
                "ik,ij->kj", w_rows[brow], ratios, preferred_element_type=jnp.float32
            )
            part_w = part_w + jnp.einsum(
                "ij,kj->ik", ratios, h_block, preferred_element_type=jnp.float32
            )
            offset = (target - row_index) % n_row
            old = lax.dynamic_index_in_dim(numer_h_stack, offset, 0, keepdims=True)
            numer_h_stack = lax.dynamic_update_index_in_dim(
                numer_h_stack, old + part_h[None], offset, 0
            )
        parts_w.append(part_w)
    numer_w = jnp.stack(parts_w).reshape(tile_rows, rank)
    return [numer_h_stack[e] for e in range(n_row)], numer_w


def body(a_blocks, block_list, block_count, w_factor, h_factor):
    values = a_blocks[0, 0]
    lists = block_list[0, 0]
    counts = block_count[0, 0]
    w_tile = w_factor[0]
    row_blocks, stored, width = values.shape[0], values.shape[1], values.shape[2]
    rank = w_tile.shape[1]
    tile_rows = w_tile.shape[0]
    n_row = lax.axis_size("row")
    n_col = lax.axis_size("col")
    n_sub = lax.axis_size("sub")
    row_index = lax.axis_index("row")
    col_index = lax.axis_index("col")

    h_stack = jnp.stack([h_factor] + [shifted(h_factor, "row", d) for d in range(1, n_row)])
    h_sum = jnp.sum(h_stack.astype(jnp.float32), axis=(0, 2))
    w_sum = jnp.sum(w_tile.astype(jnp.float32), axis=0)

    if tile_rows * n_row * width * 4 <= (8 << 20):
        numer_h_stack, numer_w = dense_terms(values, lists, counts, w_tile, h_stack, row_index)
    else:
        numer_h_stack, numer_w = slot_terms(values, lists, counts, w_tile, h_stack, row_index)

    share = tile_rows // n_col
    chunks = numer_w.reshape(n_col, share, rank)
    h_rows = as_rows(h_sum, rank)
    mine_w = lax.dynamic_index_in_dim(chunks, col_index, 0, keepdims=False)
    got_h = h_rows
    for d in range(1, n_col):
        chunk = lax.dynamic_index_in_dim(chunks, (col_index + d) % n_col, 0, keepdims=False)
        message = shifted(jnp.concatenate([chunk, h_rows]), "col", d)
        mine_w = mine_w + message[:share]
        got_h = got_h + message[share:]
    h_total = from_rows(got_h, rank)

    w_rows_sum = as_rows(w_sum, width)
    mine_h = numer_h_stack[0]
    got_w = w_rows_sum
    for d in range(1, n_row):
        message = shifted(jnp.concatenate([numer_h_stack[d], w_rows_sum]), "row", d)
        mine_h = mine_h + message[:rank]
        got_w = got_w + message[rank:]
    both = jnp.concatenate([mine_h, got_w])
    total = both
    for d in range(1, n_sub):
        total = total + shifted(both, "sub", d)
    numer_h = total[:rank]
    w_total = from_rows(total[rank:], rank)

    h_new = h_factor.astype(jnp.float32) * numer_h / w_total[:, None]
    w_part = lax.dynamic_slice_in_dim(w_tile, col_index * share, share, 0).astype(jnp.float32)
    w_new = (w_part * mine_w / h_total[None, :])[None]
    return (w_new, h_new)


def solution(mesh):
    placed = (
        P(("grp", "row", "sub"), "col", None, None, None, None),
        P(("grp", "row", "sub"), "col", None, None),
        P(("grp", "row", "sub"), "col", None),
        P(("grp", "row", "sub"), None, None),
        P(None, ("grp", "row", "col")),
    )
    return jax.shard_map(
        body,
        mesh=mesh,
        in_specs=placed,
        out_specs=(P(("grp", "row", "sub"), "col", None), P(None, ("grp", "row", "col"))),
        check_vma=False,
    )
```

```python
import jax
import jax.numpy as jnp
from jax import lax
from jax.sharding import PartitionSpec as P


def shifted(value, axis, by):
    length = lax.axis_size(axis)
    return lax.ppermute(value, axis, [(i, (i + by) % length) for i in range(length)])


def as_rows(vector, width):
    size = vector.shape[0]
    rows = -(-size // width)
    flat = jnp.pad(vector, (0, rows * width - size)).reshape(rows, width)
    return jnp.pad(flat, ((0, (-rows) % 8), (0, 0)))


def from_rows(rows, size):
    return rows.reshape(-1)[:size]


def assemble(pieces, index, count, axis):
    out = []
    for j in range(count):
        want = (index - j) % count
        chosen = pieces[0]
        for k in range(1, count):
            chosen = jnp.where(want == k, pieces[k], chosen)
        out.append(chosen)
    return jnp.concatenate(out, axis=axis)


def dense_terms(values, lists, counts, w_tile, h_stack, row_index):
    row_blocks, stored, width = values.shape[0], values.shape[1], values.shape[2]
    n_row, rank = h_stack.shape[0], h_stack.shape[1]
    tile_rows = w_tile.shape[0]
    h_all = jnp.concatenate([h_stack[d] for d in range(n_row)], axis=1)
    product = jnp.dot(w_tile, h_all, preferred_element_type=jnp.float32)
    chunks = []
    for d in range(n_row):
        block = (row_index - d) % n_row
        a_d = jnp.zeros((row_blocks, width, width), values.dtype)
        covered = jnp.zeros((row_blocks,), jnp.bool_)
        for slot in range(stored):
            match = (lists[:, slot] == block) & (slot < counts)
            a_d = jnp.where(match[:, None, None], values[:, slot], a_d)
            covered = covered | match
        p_d = product[:, d * width:(d + 1) * width].reshape(row_blocks, width, width)
        r_d = jnp.where(covered[:, None, None], a_d.astype(jnp.float32) / p_d, 0.0)
        chunks.append(r_d.astype(jnp.bfloat16).reshape(tile_rows, width))
    ratios = jnp.concatenate(chunks, axis=1)
    numer_h_all = jnp.einsum("ik,ij->kj", w_tile, ratios, preferred_element_type=jnp.float32)
    numer_w = jnp.einsum("ij,kj->ik", ratios, h_all, preferred_element_type=jnp.float32)
    starts = [((-e) % n_row) * width for e in range(n_row)]
    return [numer_h_all[:, s:s + width] for s in starts], numer_w


def slot_terms(values, lists, counts, w_tile, h_stack, row_index):
    row_blocks, stored, width = values.shape[0], values.shape[1], values.shape[2]
    n_row, rank = h_stack.shape[0], h_stack.shape[1]
    tile_rows = w_tile.shape[0]
    w_rows = w_tile.reshape(row_blocks, width, rank)
    numer_h_stack = jnp.zeros((n_row, rank, width), jnp.float32)
    parts_w = []
    for brow in range(row_blocks):
        part_w = jnp.zeros((width, rank), jnp.float32)
        for slot in range(stored):
            target = lists[brow, slot]
            live = slot < counts[brow]
            h_block = lax.dynamic_index_in_dim(
                h_stack, (row_index - target) % n_row, 0, keepdims=False
            )
            product = jnp.dot(w_rows[brow], h_block, preferred_element_type=jnp.float32)
            ratios = (values[brow, slot].astype(jnp.float32) / product).astype(jnp.bfloat16)
            ratios = jnp.where(live, ratios, jnp.zeros_like(ratios))
            part_h = jnp.einsum(
                "ik,ij->kj", w_rows[brow], ratios, preferred_element_type=jnp.float32
            )
            part_w = part_w + jnp.einsum(
                "ij,kj->ik", ratios, h_block, preferred_element_type=jnp.float32
            )
            offset = (target - row_index) % n_row
            old = lax.dynamic_index_in_dim(numer_h_stack, offset, 0, keepdims=True)
            numer_h_stack = lax.dynamic_update_index_in_dim(
                numer_h_stack, old + part_h[None], offset, 0
            )
        parts_w.append(part_w)
    numer_w = jnp.stack(parts_w).reshape(tile_rows, rank)
    return [numer_h_stack[e] for e in range(n_row)], numer_w


def body(a_blocks, block_list, block_count, w_factor, h_factor):
    values = a_blocks[0, 0]
    lists = block_list[0, 0]
    counts = block_count[0, 0]
    w_tile = w_factor[0]
    row_blocks, stored, width = values.shape[0], values.shape[1], values.shape[2]
    rank = w_tile.shape[1]
    tile_rows = w_tile.shape[0]
    n_row = lax.axis_size("row")
    n_col = lax.axis_size("col")
    n_sub = lax.axis_size("sub")
    row_index = lax.axis_index("row")
    col_index = lax.axis_index("col")

    sub_index = lax.axis_index("sub")
    half = width // n_sub
    own_piece = lax.dynamic_slice_in_dim(h_factor, sub_index * half, half, 1)
    fetched = jnp.stack([shifted(own_piece, "row", d) for d in range(1, n_row)])
    swapped = [fetched] + [shifted(fetched, "sub", k) for k in range(1, n_sub)]
    others = assemble(swapped, sub_index, n_sub, 2)
    h_stack = jnp.concatenate([h_factor[None], others])
    h_sum = jnp.sum(h_stack.astype(jnp.float32), axis=(0, 2))
    w_sum = jnp.sum(w_tile.astype(jnp.float32), axis=0)

    if tile_rows * n_row * width * 4 <= (8 << 20):
        numer_h_stack, numer_w = dense_terms(values, lists, counts, w_tile, h_stack, row_index)
    else:
        numer_h_stack, numer_w = slot_terms(values, lists, counts, w_tile, h_stack, row_index)

    share = tile_rows // n_col
    chunks = numer_w.reshape(n_col, share, rank)
    h_rows = as_rows(h_sum, rank)
    mine_w = lax.dynamic_index_in_dim(chunks, col_index, 0, keepdims=False)
    got_h = h_rows
    for d in range(1, n_col):
        chunk = lax.dynamic_index_in_dim(chunks, (col_index + d) % n_col, 0, keepdims=False)
        message = shifted(jnp.concatenate([chunk, h_rows]), "col", d)
        mine_w = mine_w + message[:share]
        got_h = got_h + message[share:]
    h_total = from_rows(got_h, rank)

    w_rows_sum = as_rows(w_sum, width)
    def piece_message(p):
        return jnp.concatenate(
            [lax.dynamic_slice_in_dim(x, p * half, half, 1) for x in numer_h_stack + [w_rows_sum]]
        )
    reduced = piece_message(sub_index)
    for k in range(1, n_sub):
        reduced = reduced + shifted(piece_message((sub_index + k) % n_sub), "sub", k)
    extra = reduced[n_row * rank:]
    mine_h = reduced[:rank]
    got_w = extra
    for d in range(1, n_row):
        message = shifted(jnp.concatenate([reduced[d * rank:(d + 1) * rank], extra]), "row", d)
        mine_h = mine_h + message[:rank]
        got_w = got_w + message[rank:]
    final = jnp.concatenate([mine_h, got_w])
    total = assemble([final] + [shifted(final, "sub", k) for k in range(1, n_sub)], sub_index, n_sub, 1)
    numer_h = total[:rank]
    w_total = from_rows(total[rank:], rank)

    h_new = h_factor.astype(jnp.float32) * numer_h / w_total[:, None]
    w_part = lax.dynamic_slice_in_dim(w_tile, col_index * share, share, 0).astype(jnp.float32)
    w_new = (w_part * mine_w / h_total[None, :])[None]
    return (w_new, h_new)


def solution(mesh):
    placed = (
        P(("grp", "row", "sub"), "col", None, None, None, None),
        P(("grp", "row", "sub"), "col", None, None),
        P(("grp", "row", "sub"), "col", None),
        P(("grp", "row", "sub"), None, None),
        P(None, ("grp", "row", "col")),
    )
    return jax.shard_map(
        body,
        mesh=mesh,
        in_specs=placed,
        out_specs=(P(("grp", "row", "sub"), "col", None), P(None, ("grp", "row", "col"))),
        check_vma=False,
    )
```

```python
import jax
import jax.numpy as jnp
from jax import lax
from jax.sharding import PartitionSpec as P


def shifted(value, axis, by):
    length = lax.axis_size(axis)
    return lax.ppermute(value, axis, [(i, (i + by) % length) for i in range(length)])


def as_rows(vector, width):
    size = vector.shape[0]
    rows = -(-size // width)
    flat = jnp.pad(vector, (0, rows * width - size)).reshape(rows, width)
    return jnp.pad(flat, ((0, (-rows) % 8), (0, 0)))


def from_rows(rows, size):
    return rows.reshape(-1)[:size]


def assemble(pieces, index, count, axis):
    out = []
    for j in range(count):
        want = (index - j) % count
        chosen = pieces[0]
        for k in range(1, count):
            chosen = jnp.where(want == k, pieces[k], chosen)
        out.append(chosen)
    return jnp.concatenate(out, axis=axis)


def dense_terms(values, lists, counts, w_tile, h_stack, row_index):
    row_blocks, stored, width = values.shape[0], values.shape[1], values.shape[2]
    n_row, rank = h_stack.shape[0], h_stack.shape[1]
    tile_rows = w_tile.shape[0]
    h_all = jnp.concatenate([h_stack[d] for d in range(n_row)], axis=1)
    product = jnp.dot(w_tile, h_all, preferred_element_type=jnp.float32)
    chunks = []
    for d in range(n_row):
        block = (row_index - d) % n_row
        a_d = jnp.zeros((row_blocks, width, width), values.dtype)
        covered = jnp.zeros((row_blocks,), jnp.bool_)
        for slot in range(stored):
            match = (lists[:, slot] == block) & (slot < counts)
            a_d = jnp.where(match[:, None, None], values[:, slot], a_d)
            covered = covered | match
        p_d = product[:, d * width:(d + 1) * width].reshape(row_blocks, width, width)
        r_d = jnp.where(covered[:, None, None], a_d.astype(jnp.float32) / p_d, 0.0)
        chunks.append(r_d.astype(jnp.bfloat16).reshape(tile_rows, width))
    ratios = jnp.concatenate(chunks, axis=1)
    numer_h_all = jnp.einsum("ik,ij->kj", w_tile, ratios, preferred_element_type=jnp.float32)
    numer_w = jnp.einsum("ij,kj->ik", ratios, h_all, preferred_element_type=jnp.float32)
    starts = [((-e) % n_row) * width for e in range(n_row)]
    return [numer_h_all[:, s:s + width] for s in starts], numer_w


def slot_terms(values, lists, counts, w_tile, h_stack, row_index):
    row_blocks, stored, width = values.shape[0], values.shape[1], values.shape[2]
    n_row, rank = h_stack.shape[0], h_stack.shape[1]
    tile_rows = w_tile.shape[0]
    w_rows = w_tile.reshape(row_blocks, width, rank)
    numer_h_stack = jnp.zeros((n_row, rank, width), jnp.float32)
    parts_w = []
    for brow in range(row_blocks):
        part_w = jnp.zeros((width, rank), jnp.float32)
        for slot in range(stored):
            target = lists[brow, slot]
            live = slot < counts[brow]
            h_block = lax.dynamic_index_in_dim(
                h_stack, (row_index - target) % n_row, 0, keepdims=False
            )
            product = jnp.dot(w_rows[brow], h_block, preferred_element_type=jnp.float32)
            ratios = (values[brow, slot].astype(jnp.float32) / product).astype(jnp.bfloat16)
            ratios = jnp.where(live, ratios, jnp.zeros_like(ratios))
            part_h = jnp.einsum(
                "ik,ij->kj", w_rows[brow], ratios, preferred_element_type=jnp.float32
            )
            part_w = part_w + jnp.einsum(
                "ij,kj->ik", ratios, h_block, preferred_element_type=jnp.float32
            )
            offset = (target - row_index) % n_row
            old = lax.dynamic_index_in_dim(numer_h_stack, offset, 0, keepdims=True)
            numer_h_stack = lax.dynamic_update_index_in_dim(
                numer_h_stack, old + part_h[None], offset, 0
            )
        parts_w.append(part_w)
    numer_w = jnp.stack(parts_w).reshape(tile_rows, rank)
    return [numer_h_stack[e] for e in range(n_row)], numer_w


def body(a_blocks, block_list, block_count, w_factor, h_factor):
    values = a_blocks[0, 0]
    lists = block_list[0, 0]
    counts = block_count[0, 0]
    w_tile = w_factor[0]
    row_blocks, stored, width = values.shape[0], values.shape[1], values.shape[2]
    rank = w_tile.shape[1]
    tile_rows = w_tile.shape[0]
    n_row = lax.axis_size("row")
    n_col = lax.axis_size("col")
    n_sub = lax.axis_size("sub")
    row_index = lax.axis_index("row")
    col_index = lax.axis_index("col")

    sub_index = lax.axis_index("sub")
    half = width // n_sub
    own_piece = lax.dynamic_slice_in_dim(h_factor, sub_index * half, half, 1)
    fetched = jnp.stack([shifted(own_piece, "row", d) for d in range(1, n_row)])
    swapped = [fetched] + [shifted(fetched, "sub", k) for k in range(1, n_sub)]
    others = assemble(swapped, sub_index, n_sub, 2)
    h_stack = jnp.concatenate([h_factor[None], others])
    h_sum = jnp.sum(h_stack.astype(jnp.float32), axis=(0, 2))
    w_sum = jnp.sum(w_tile.astype(jnp.float32), axis=0)

    if tile_rows * n_row * width * 4 <= (8 << 20):
        numer_h_stack, numer_w = dense_terms(values, lists, counts, w_tile, h_stack, row_index)
    else:
        numer_h_stack, numer_w = slot_terms(values, lists, counts, w_tile, h_stack, row_index)

    share = tile_rows // n_col
    chunks = numer_w.reshape(n_col, share, rank)
    h_rows = as_rows(h_sum, rank)
    mine_w = lax.dynamic_index_in_dim(chunks, col_index, 0, keepdims=False)
    got_h = h_rows
    for d in range(1, n_col):
        chunk = lax.dynamic_index_in_dim(chunks, (col_index + d) % n_col, 0, keepdims=False)
        message = shifted(jnp.concatenate([chunk, h_rows]), "col", d)
        mine_w = mine_w + message[:share]
        got_h = got_h + message[share:]
    h_total = from_rows(got_h, rank)

    w_rows_sum = as_rows(w_sum, width)
    messages = [
        jnp.concatenate([x[:, p * half:(p + 1) * half] for x in numer_h_stack + [w_rows_sum]])
        for p in range(n_sub)
    ]
    def piece_message(k):
        want = (sub_index + k) % n_sub
        chosen = messages[0]
        for p in range(1, n_sub):
            chosen = jnp.where(want == p, messages[p], chosen)
        return chosen
    reduced = piece_message(0)
    for k in range(1, n_sub):
        reduced = reduced + shifted(piece_message(k), "sub", k)
    extra = reduced[n_row * rank:]
    mine_h = reduced[:rank]
    got_w = extra
    for d in range(1, n_row):
        message = shifted(jnp.concatenate([reduced[d * rank:(d + 1) * rank], extra]), "row", d)
        mine_h = mine_h + message[:rank]
        got_w = got_w + message[rank:]
    final = jnp.concatenate([mine_h, got_w])
    total = assemble([final] + [shifted(final, "sub", k) for k in range(1, n_sub)], sub_index, n_sub, 1)
    numer_h = total[:rank]
    w_total = from_rows(total[rank:], rank)

    h_new = h_factor.astype(jnp.float32) * numer_h / w_total[:, None]
    w_part = lax.dynamic_slice_in_dim(w_tile, col_index * share, share, 0).astype(jnp.float32)
    w_new = (w_part * mine_w / h_total[None, :])[None]
    return (w_new, h_new)


def solution(mesh):
    placed = (
        P(("grp", "row", "sub"), "col", None, None, None, None),
        P(("grp", "row", "sub"), "col", None, None),
        P(("grp", "row", "sub"), "col", None),
        P(("grp", "row", "sub"), None, None),
        P(None, ("grp", "row", "col")),
    )
    return jax.shard_map(
        body,
        mesh=mesh,
        in_specs=placed,
        out_specs=(P(("grp", "row", "sub"), "col", None), P(None, ("grp", "row", "col"))),
        check_vma=False,
    )
```

```python
import jax
import jax.numpy as jnp
from jax import lax
from jax.sharding import PartitionSpec as P


def shifted(value, axis, by):
    length = lax.axis_size(axis)
    return lax.ppermute(value, axis, [(i, (i + by) % length) for i in range(length)])


def as_rows(vector, width):
    size = vector.shape[0]
    rows = -(-size // width)
    flat = jnp.pad(vector, (0, rows * width - size)).reshape(rows, width)
    return jnp.pad(flat, ((0, (-rows) % 8), (0, 0)))


def from_rows(rows, size):
    return rows.reshape(-1)[:size]


def assemble(pieces, index, count, axis):
    out = []
    for j in range(count):
        want = (index - j) % count
        chosen = pieces[0]
        for k in range(1, count):
            chosen = jnp.where(want == k, pieces[k], chosen)
        out.append(chosen)
    return jnp.concatenate(out, axis=axis)


def dense_terms(values, lists, counts, w_tile, h_stack, row_index):
    row_blocks, stored, width = values.shape[0], values.shape[1], values.shape[2]
    n_row, rank = h_stack.shape[0], h_stack.shape[1]
    tile_rows = w_tile.shape[0]
    h_all = jnp.concatenate([h_stack[d] for d in range(n_row)], axis=1)
    product = jnp.dot(w_tile, h_all, preferred_element_type=jnp.float32)
    chunks = []
    for d in range(n_row):
        block = (row_index - d) % n_row
        a_d = jnp.zeros((row_blocks, width, width), values.dtype)
        covered = jnp.zeros((row_blocks,), jnp.bool_)
        for slot in range(stored):
            match = (lists[:, slot] == block) & (slot < counts)
            a_d = jnp.where(match[:, None, None], values[:, slot], a_d)
            covered = covered | match
        p_d = product[:, d * width:(d + 1) * width].reshape(row_blocks, width, width)
        r_d = jnp.where(covered[:, None, None], a_d.astype(jnp.float32) / p_d, 0.0)
        chunks.append(r_d.astype(jnp.bfloat16).reshape(tile_rows, width))
    ratios = jnp.concatenate(chunks, axis=1)
    numer_h_all = jnp.einsum("ik,ij->kj", w_tile, ratios, preferred_element_type=jnp.float32)
    numer_w = jnp.einsum("ij,kj->ik", ratios, h_all, preferred_element_type=jnp.float32)
    starts = [((-e) % n_row) * width for e in range(n_row)]
    return [numer_h_all[:, s:s + width] for s in starts], numer_w


def slot_terms(values, lists, counts, w_tile, h_stack, row_index):
    row_blocks, stored, width = values.shape[0], values.shape[1], values.shape[2]
    n_row, rank = h_stack.shape[0], h_stack.shape[1]
    tile_rows = w_tile.shape[0]
    w_rows = w_tile.reshape(row_blocks, width, rank)
    numer_h_stack = jnp.zeros((n_row, rank, width), jnp.float32)
    parts_w = []
    for brow in range(row_blocks):
        part_w = jnp.zeros((width, rank), jnp.float32)
        for slot in range(stored):
            target = lists[brow, slot]
            live = slot < counts[brow]
            h_block = lax.dynamic_index_in_dim(
                h_stack, (row_index - target) % n_row, 0, keepdims=False
            )
            product = jnp.dot(w_rows[brow], h_block, preferred_element_type=jnp.float32)
            ratios = (values[brow, slot].astype(jnp.float32) / product).astype(jnp.bfloat16)
            ratios = jnp.where(live, ratios, jnp.zeros_like(ratios))
            part_h = jnp.einsum(
                "ik,ij->kj", w_rows[brow], ratios, preferred_element_type=jnp.float32
            )
            part_w = part_w + jnp.einsum(
                "ij,kj->ik", ratios, h_block, preferred_element_type=jnp.float32
            )
            offset = (target - row_index) % n_row
            old = lax.dynamic_index_in_dim(numer_h_stack, offset, 0, keepdims=True)
            numer_h_stack = lax.dynamic_update_index_in_dim(
                numer_h_stack, old + part_h[None], offset, 0
            )
        parts_w.append(part_w)
    numer_w = jnp.stack(parts_w).reshape(tile_rows, rank)
    return [numer_h_stack[e] for e in range(n_row)], numer_w


def body(a_blocks, block_list, block_count, w_factor, h_factor):
    values = a_blocks[0, 0]
    lists = block_list[0, 0]
    counts = block_count[0, 0]
    w_tile = w_factor[0]
    row_blocks, stored, width = values.shape[0], values.shape[1], values.shape[2]
    rank = w_tile.shape[1]
    tile_rows = w_tile.shape[0]
    n_row = lax.axis_size("row")
    n_col = lax.axis_size("col")
    n_sub = lax.axis_size("sub")
    row_index = lax.axis_index("row")
    col_index = lax.axis_index("col")

    sub_index = lax.axis_index("sub")
    half = width // n_sub
    own_piece = lax.dynamic_slice_in_dim(h_factor, sub_index * half, half, 1)
    fetched = jnp.stack([shifted(own_piece, "row", d) for d in range(1, n_row)])
    swapped = [fetched] + [shifted(fetched, "sub", k) for k in range(1, n_sub)]
    others = assemble(swapped, sub_index, n_sub, 2)
    h_stack = jnp.concatenate([h_factor[None], others])
    h_sum = jnp.sum(h_stack.astype(jnp.float32), axis=(0, 2))
    w_sum = jnp.sum(w_tile.astype(jnp.float32), axis=0)

    if tile_rows * n_row * width * 4 <= (8 << 20):
        numer_h_stack, numer_w = dense_terms(values, lists, counts, w_tile, h_stack, row_index)
    else:
        numer_h_stack, numer_w = slot_terms(values, lists, counts, w_tile, h_stack, row_index)

    share = tile_rows // n_col
    chunks = numer_w.reshape(n_col, share, rank)
    h_rows = as_rows(h_sum, rank)
    mine_w = lax.dynamic_index_in_dim(chunks, col_index, 0, keepdims=False)
    got_h = h_rows
    for d in range(1, n_col):
        chunk = lax.dynamic_index_in_dim(chunks, (col_index + d) % n_col, 0, keepdims=False)
        cut = share // 2
        first = shifted(chunk[:cut], "col", d)
        second = shifted(jnp.concatenate([chunk[cut:], h_rows]), "col", d)
        mine_w = mine_w + jnp.concatenate([first, second[:share - cut]])
        got_h = got_h + second[share - cut:]
    h_total = from_rows(got_h, rank)

    w_rows_sum = as_rows(w_sum, width)
    messages = [
        jnp.concatenate([x[:, p * half:(p + 1) * half] for x in numer_h_stack + [w_rows_sum]])
        for p in range(n_sub)
    ]
    def piece_message(k):
        want = (sub_index + k) % n_sub
        chosen = messages[0]
        for p in range(1, n_sub):
            chosen = jnp.where(want == p, messages[p], chosen)
        return chosen
    reduced = piece_message(0)
    for k in range(1, n_sub):
        reduced = reduced + shifted(piece_message(k), "sub", k)
    extra = reduced[n_row * rank:]
    mine_h = reduced[:rank]
    got_w = extra
    for d in range(1, n_row):
        message = shifted(jnp.concatenate([reduced[d * rank:(d + 1) * rank], extra]), "row", d)
        mine_h = mine_h + message[:rank]
        got_w = got_w + message[rank:]
    final = jnp.concatenate([mine_h, got_w])
    total = assemble([final] + [shifted(final, "sub", k) for k in range(1, n_sub)], sub_index, n_sub, 1)
    numer_h = total[:rank]
    w_total = from_rows(total[rank:], rank)

    h_new = h_factor.astype(jnp.float32) * numer_h / w_total[:, None]
    w_part = lax.dynamic_slice_in_dim(w_tile, col_index * share, share, 0).astype(jnp.float32)
    w_new = (w_part * mine_w / h_total[None, :])[None]
    return (w_new, h_new)


def solution(mesh):
    placed = (
        P(("grp", "row", "sub"), "col", None, None, None, None),
        P(("grp", "row", "sub"), "col", None, None),
        P(("grp", "row", "sub"), "col", None),
        P(("grp", "row", "sub"), None, None),
        P(None, ("grp", "row", "col")),
    )
    return jax.shard_map(
        body,
        mesh=mesh,
        in_specs=placed,
        out_specs=(P(("grp", "row", "sub"), "col", None), P(None, ("grp", "row", "col"))),
        check_vma=False,
    )
```

```python
import jax
import jax.numpy as jnp
from jax import lax
from jax.sharding import PartitionSpec as P


def shifted(value, axis, by):
    length = lax.axis_size(axis)
    return lax.ppermute(value, axis, [(i, (i + by) % length) for i in range(length)])


def as_rows(vector, width):
    size = vector.shape[0]
    rows = -(-size // width)
    flat = jnp.pad(vector, (0, rows * width - size)).reshape(rows, width)
    return jnp.pad(flat, ((0, (-rows) % 8), (0, 0)))


def from_rows(rows, size):
    return rows.reshape(-1)[:size]


def assemble(pieces, index, count, axis):
    out = []
    for j in range(count):
        want = (index - j) % count
        chosen = pieces[0]
        for k in range(1, count):
            chosen = jnp.where(want == k, pieces[k], chosen)
        out.append(chosen)
    return jnp.concatenate(out, axis=axis)


def dense_terms(values, lists, counts, w_tile, h_stack, row_index):
    row_blocks, stored, width = values.shape[0], values.shape[1], values.shape[2]
    n_row, rank = h_stack.shape[0], h_stack.shape[1]
    tile_rows = w_tile.shape[0]
    h_all = jnp.concatenate([h_stack[d] for d in range(n_row)], axis=1)
    product = jnp.dot(w_tile, h_all, preferred_element_type=jnp.float32)
    chunks = []
    for d in range(n_row):
        block = (row_index - d) % n_row
        a_d = jnp.zeros((row_blocks, width, width), values.dtype)
        covered = jnp.zeros((row_blocks,), jnp.bool_)
        for slot in range(stored):
            match = (lists[:, slot] == block) & (slot < counts)
            a_d = jnp.where(match[:, None, None], values[:, slot], a_d)
            covered = covered | match
        p_d = product[:, d * width:(d + 1) * width].reshape(row_blocks, width, width)
        r_d = jnp.where(covered[:, None, None], a_d.astype(jnp.float32) / p_d, 0.0)
        chunks.append(r_d.astype(jnp.bfloat16).reshape(tile_rows, width))
    ratios = jnp.concatenate(chunks, axis=1)
    numer_h_all = jnp.einsum("ik,ij->kj", w_tile, ratios, preferred_element_type=jnp.float32)
    numer_w = jnp.einsum("ij,kj->ik", ratios, h_all, preferred_element_type=jnp.float32)
    starts = [((-e) % n_row) * width for e in range(n_row)]
    return [numer_h_all[:, s:s + width] for s in starts], numer_w


def slot_terms(values, lists, counts, w_tile, h_stack, row_index):
    row_blocks, stored, width = values.shape[0], values.shape[1], values.shape[2]
    n_row, rank = h_stack.shape[0], h_stack.shape[1]
    tile_rows = w_tile.shape[0]
    w_rows = w_tile.reshape(row_blocks, width, rank)
    numer_h_stack = jnp.zeros((n_row, rank, width), jnp.float32)
    parts_w = []
    for brow in range(row_blocks):
        part_w = jnp.zeros((width, rank), jnp.float32)
        for slot in range(stored):
            target = lists[brow, slot]
            live = slot < counts[brow]
            h_block = lax.dynamic_index_in_dim(
                h_stack, (row_index - target) % n_row, 0, keepdims=False
            )
            product = jnp.dot(w_rows[brow], h_block, preferred_element_type=jnp.float32)
            ratios = (values[brow, slot].astype(jnp.float32) / product).astype(jnp.bfloat16)
            ratios = jnp.where(live, ratios, jnp.zeros_like(ratios))
            part_h = jnp.einsum(
                "ik,ij->kj", w_rows[brow], ratios, preferred_element_type=jnp.float32
            )
            part_w = part_w + jnp.einsum(
                "ij,kj->ik", ratios, h_block, preferred_element_type=jnp.float32
            )
            offset = (target - row_index) % n_row
            old = lax.dynamic_index_in_dim(numer_h_stack, offset, 0, keepdims=True)
            numer_h_stack = lax.dynamic_update_index_in_dim(
                numer_h_stack, old + part_h[None], offset, 0
            )
        parts_w.append(part_w)
    numer_w = jnp.stack(parts_w).reshape(tile_rows, rank)
    return [numer_h_stack[e] for e in range(n_row)], numer_w


def body(a_blocks, block_list, block_count, w_factor, h_factor):
    values = a_blocks[0, 0]
    lists = block_list[0, 0]
    counts = block_count[0, 0]
    w_tile = w_factor[0]
    row_blocks, stored, width = values.shape[0], values.shape[1], values.shape[2]
    rank = w_tile.shape[1]
    tile_rows = w_tile.shape[0]
    n_row = lax.axis_size("row")
    n_col = lax.axis_size("col")
    n_sub = lax.axis_size("sub")
    row_index = lax.axis_index("row")
    col_index = lax.axis_index("col")

    sub_index = lax.axis_index("sub")
    half = width // n_sub
    own_piece = lax.dynamic_slice_in_dim(h_factor, sub_index * half, half, 1)
    fetched = jnp.stack([shifted(own_piece, "row", d) for d in range(1, n_row)])
    swapped = [fetched] + [shifted(fetched, "sub", k) for k in range(1, n_sub)]
    others = assemble(swapped, sub_index, n_sub, 2)
    h_stack = jnp.concatenate([h_factor[None], others])
    h_sum = jnp.sum(h_stack.astype(jnp.float32), axis=(0, 2))
    w_sum = jnp.sum(w_tile.astype(jnp.float32), axis=0)

    if tile_rows * n_row * width * 4 <= (8 << 20):
        numer_h_stack, numer_w = dense_terms(values, lists, counts, w_tile, h_stack, row_index)
    else:
        numer_h_stack, numer_w = slot_terms(values, lists, counts, w_tile, h_stack, row_index)

    share = tile_rows // n_col
    chunks = numer_w.reshape(n_col, share, rank)
    h_rows = as_rows(h_sum, rank)
    mine_w = lax.dynamic_index_in_dim(chunks, col_index, 0, keepdims=False)
    got_h = h_rows
    for d in range(1, n_col):
        chunk = lax.dynamic_index_in_dim(chunks, (col_index + d) % n_col, 0, keepdims=False)
        message = shifted(jnp.concatenate([chunk, h_rows]), "col", d)
        mine_w = mine_w + message[:share]
        got_h = got_h + message[share:]
    h_total = from_rows(got_h, rank)

    w_rows_sum = as_rows(w_sum, width)
    messages = [
        jnp.concatenate([x[:, p * half:(p + 1) * half] for x in numer_h_stack + [w_rows_sum]])
        for p in range(n_sub)
    ]
    def piece_message(k):
        want = (sub_index + k) % n_sub
        chosen = messages[0]
        for p in range(1, n_sub):
            chosen = jnp.where(want == p, messages[p], chosen)
        return chosen
    reduced = piece_message(0)
    for k in range(1, n_sub):
        reduced = reduced + shifted(piece_message(k), "sub", k)
    extra = reduced[n_row * rank:]
    outgoing = jnp.stack(
        [jnp.concatenate([reduced[e * rank:(e + 1) * rank], extra]) for e in range(n_row)]
    )
    doubled = jnp.concatenate([outgoing, outgoing])
    outgoing = lax.dynamic_slice_in_dim(doubled, n_row - row_index, n_row, 0)
    incoming = lax.all_to_all(outgoing, "row", 0, 0, tiled=True)
    final = jnp.sum(incoming, axis=0)
    total = assemble([final] + [shifted(final, "sub", k) for k in range(1, n_sub)], sub_index, n_sub, 1)
    numer_h = total[:rank]
    w_total = from_rows(total[rank:], rank)

    h_new = h_factor.astype(jnp.float32) * numer_h / w_total[:, None]
    w_part = lax.dynamic_slice_in_dim(w_tile, col_index * share, share, 0).astype(jnp.float32)
    w_new = (w_part * mine_w / h_total[None, :])[None]
    return (w_new, h_new)


def solution(mesh):
    placed = (
        P(("grp", "row", "sub"), "col", None, None, None, None),
        P(("grp", "row", "sub"), "col", None, None),
        P(("grp", "row", "sub"), "col", None),
        P(("grp", "row", "sub"), None, None),
        P(None, ("grp", "row", "col")),
    )
    return jax.shard_map(
        body,
        mesh=mesh,
        in_specs=placed,
        out_specs=(P(("grp", "row", "sub"), "col", None), P(None, ("grp", "row", "col"))),
        check_vma=False,
    )
```

```python
import jax
import jax.numpy as jnp
from jax import lax
from jax.sharding import PartitionSpec as P


def shifted(value, axis, by):
    length = lax.axis_size(axis)
    return lax.ppermute(value, axis, [(i, (i + by) % length) for i in range(length)])


def as_rows(vector, width):
    size = vector.shape[0]
    rows = -(-size // width)
    flat = jnp.pad(vector, (0, rows * width - size)).reshape(rows, width)
    return jnp.pad(flat, ((0, (-rows) % 8), (0, 0)))


def from_rows(rows, size):
    return rows.reshape(-1)[:size]


def assemble(pieces, index, count, axis):
    out = []
    for j in range(count):
        want = (index - j) % count
        chosen = pieces[0]
        for k in range(1, count):
            chosen = jnp.where(want == k, pieces[k], chosen)
        out.append(chosen)
    return jnp.concatenate(out, axis=axis)


def dense_terms(values, lists, counts, w_tile, h_stack, row_index):
    row_blocks, stored, width = values.shape[0], values.shape[1], values.shape[2]
    n_row, rank = h_stack.shape[0], h_stack.shape[1]
    tile_rows = w_tile.shape[0]
    h_all = jnp.concatenate([h_stack[d] for d in range(n_row)], axis=1)
    product = jnp.dot(w_tile, h_all, preferred_element_type=jnp.float32)
    chunks = []
    for d in range(n_row):
        block = (row_index - d) % n_row
        a_d = jnp.zeros((row_blocks, width, width), values.dtype)
        covered = jnp.zeros((row_blocks,), jnp.bool_)
        for slot in range(stored):
            match = (lists[:, slot] == block) & (slot < counts)
            a_d = jnp.where(match[:, None, None], values[:, slot], a_d)
            covered = covered | match
        p_d = product[:, d * width:(d + 1) * width].reshape(row_blocks, width, width)
        r_d = jnp.where(covered[:, None, None], a_d.astype(jnp.float32) / p_d, 0.0)
        chunks.append(r_d.astype(jnp.bfloat16).reshape(tile_rows, width))
    ratios = jnp.concatenate(chunks, axis=1)
    numer_h_all = jnp.einsum("ik,ij->kj", w_tile, ratios, preferred_element_type=jnp.float32)
    numer_w = jnp.einsum("ij,kj->ik", ratios, h_all, preferred_element_type=jnp.float32)
    starts = [((-e) % n_row) * width for e in range(n_row)]
    return [numer_h_all[:, s:s + width] for s in starts], numer_w


def slot_terms(values, lists, counts, w_tile, h_stack, row_index):
    row_blocks, stored, width = values.shape[0], values.shape[1], values.shape[2]
    n_row, rank = h_stack.shape[0], h_stack.shape[1]
    tile_rows = w_tile.shape[0]
    w_rows = w_tile.reshape(row_blocks, width, rank)
    numer_h_stack = jnp.zeros((n_row, rank, width), jnp.float32)
    parts_w = []
    for brow in range(row_blocks):
        part_w = jnp.zeros((width, rank), jnp.float32)
        for slot in range(stored):
            target = lists[brow, slot]
            live = slot < counts[brow]
            h_block = lax.dynamic_index_in_dim(
                h_stack, (row_index - target) % n_row, 0, keepdims=False
            )
            product = jnp.dot(w_rows[brow], h_block, preferred_element_type=jnp.float32)
            ratios = (values[brow, slot].astype(jnp.float32) / product).astype(jnp.bfloat16)
            ratios = jnp.where(live, ratios, jnp.zeros_like(ratios))
            part_h = jnp.einsum(
                "ik,ij->kj", w_rows[brow], ratios, preferred_element_type=jnp.float32
            )
            part_w = part_w + jnp.einsum(
                "ij,kj->ik", ratios, h_block, preferred_element_type=jnp.float32
            )
            offset = (target - row_index) % n_row
            old = lax.dynamic_index_in_dim(numer_h_stack, offset, 0, keepdims=True)
            numer_h_stack = lax.dynamic_update_index_in_dim(
                numer_h_stack, old + part_h[None], offset, 0
            )
        parts_w.append(part_w)
    numer_w = jnp.stack(parts_w).reshape(tile_rows, rank)
    return [numer_h_stack[e] for e in range(n_row)], numer_w


def body(a_blocks, block_list, block_count, w_factor, h_factor):
    values = a_blocks[0, 0]
    lists = block_list[0, 0]
    counts = block_count[0, 0]
    w_tile = w_factor[0]
    row_blocks, stored, width = values.shape[0], values.shape[1], values.shape[2]
    rank = w_tile.shape[1]
    tile_rows = w_tile.shape[0]
    n_row = lax.axis_size("row")
    n_col = lax.axis_size("col")
    n_sub = lax.axis_size("sub")
    row_index = lax.axis_index("row")
    col_index = lax.axis_index("col")

    sub_index = lax.axis_index("sub")
    half = width // n_sub
    own_piece = lax.dynamic_slice_in_dim(h_factor, sub_index * half, half, 1)
    arrived = {d: shifted(own_piece, "row", d) for d in reversed(range(1, n_row))}
    fetched = jnp.stack([arrived[d] for d in range(1, n_row)])
    swapped = [fetched] + [shifted(fetched, "sub", k) for k in range(1, n_sub)]
    others = assemble(swapped, sub_index, n_sub, 2)
    h_stack = jnp.concatenate([h_factor[None], others])
    h_sum = jnp.sum(h_stack.astype(jnp.float32), axis=(0, 2))
    w_sum = jnp.sum(w_tile.astype(jnp.float32), axis=0)

    if tile_rows * n_row * width * 4 <= (8 << 20):
        numer_h_stack, numer_w = dense_terms(values, lists, counts, w_tile, h_stack, row_index)
    else:
        numer_h_stack, numer_w = slot_terms(values, lists, counts, w_tile, h_stack, row_index)

    share = tile_rows // n_col
    chunks = numer_w.reshape(n_col, share, rank)
    h_rows = as_rows(h_sum, rank)
    mine_w = lax.dynamic_index_in_dim(chunks, col_index, 0, keepdims=False)
    got_h = h_rows
    for d in range(1, n_col):
        chunk = lax.dynamic_index_in_dim(chunks, (col_index + d) % n_col, 0, keepdims=False)
        message = shifted(jnp.concatenate([chunk, h_rows]), "col", d)
        mine_w = mine_w + message[:share]
        got_h = got_h + message[share:]
    h_total = from_rows(got_h, rank)

    w_rows_sum = as_rows(w_sum, width)
    messages = [
        jnp.concatenate([x[:, p * half:(p + 1) * half] for x in numer_h_stack + [w_rows_sum]])
        for p in range(n_sub)
    ]
    def piece_message(k):
        want = (sub_index + k) % n_sub
        chosen = messages[0]
        for p in range(1, n_sub):
            chosen = jnp.where(want == p, messages[p], chosen)
        return chosen
    reduced = piece_message(0)
    for k in range(1, n_sub):
        reduced = reduced + shifted(piece_message(k), "sub", k)
    extra = reduced[n_row * rank:]
    mine_h = reduced[:rank]
    got_w = extra
    for d in reversed(range(1, n_row)):
        message = shifted(jnp.concatenate([reduced[d * rank:(d + 1) * rank], extra]), "row", d)
        mine_h = mine_h + message[:rank]
        got_w = got_w + message[rank:]
    final = jnp.concatenate([mine_h, got_w])
    total = assemble([final] + [shifted(final, "sub", k) for k in range(1, n_sub)], sub_index, n_sub, 1)
    numer_h = total[:rank]
    w_total = from_rows(total[rank:], rank)

    h_new = h_factor.astype(jnp.float32) * numer_h / w_total[:, None]
    w_part = lax.dynamic_slice_in_dim(w_tile, col_index * share, share, 0).astype(jnp.float32)
    w_new = (w_part * mine_w / h_total[None, :])[None]
    return (w_new, h_new)


def solution(mesh):
    placed = (
        P(("grp", "row", "sub"), "col", None, None, None, None),
        P(("grp", "row", "sub"), "col", None, None),
        P(("grp", "row", "sub"), "col", None),
        P(("grp", "row", "sub"), None, None),
        P(None, ("grp", "row", "col")),
    )
    return jax.shard_map(
        body,
        mesh=mesh,
        in_specs=placed,
        out_specs=(P(("grp", "row", "sub"), "col", None), P(None, ("grp", "row", "col"))),
        check_vma=False,
    )
```

```python
import jax
import jax.numpy as jnp
from jax import lax
from jax.sharding import PartitionSpec as P


def shifted(value, axis, by):
    length = lax.axis_size(axis)
    return lax.ppermute(value, axis, [(i, (i + by) % length) for i in range(length)])


def as_rows(vector, width):
    size = vector.shape[0]
    rows = -(-size // width)
    flat = jnp.pad(vector, (0, rows * width - size)).reshape(rows, width)
    return jnp.pad(flat, ((0, (-rows) % 8), (0, 0)))


def from_rows(rows, size):
    return rows.reshape(-1)[:size]


def assemble(pieces, index, count, axis):
    out = []
    for j in range(count):
        want = (index - j) % count
        chosen = pieces[0]
        for k in range(1, count):
            chosen = jnp.where(want == k, pieces[k], chosen)
        out.append(chosen)
    return jnp.concatenate(out, axis=axis)


def dense_terms(values, lists, counts, w_tile, h_stack, row_index):
    row_blocks, stored, width = values.shape[0], values.shape[1], values.shape[2]
    n_row, rank = h_stack.shape[0], h_stack.shape[1]
    tile_rows = w_tile.shape[0]
    h_all = jnp.concatenate([h_stack[d] for d in range(n_row)], axis=1)
    product = jnp.dot(w_tile, h_all, preferred_element_type=jnp.float32)
    chunks = []
    for d in range(n_row):
        block = (row_index - d) % n_row
        a_d = jnp.zeros((row_blocks, width, width), values.dtype)
        covered = jnp.zeros((row_blocks,), jnp.bool_)
        for slot in range(stored):
            match = (lists[:, slot] == block) & (slot < counts)
            a_d = jnp.where(match[:, None, None], values[:, slot], a_d)
            covered = covered | match
        p_d = product[:, d * width:(d + 1) * width].reshape(row_blocks, width, width)
        r_d = jnp.where(covered[:, None, None], a_d.astype(jnp.float32) / p_d, 0.0)
        chunks.append(r_d.astype(jnp.bfloat16).reshape(tile_rows, width))
    ratios = jnp.concatenate(chunks, axis=1)
    numer_h_all = jnp.einsum("ik,ij->kj", w_tile, ratios, preferred_element_type=jnp.float32)
    numer_w = jnp.einsum("ij,kj->ik", ratios, h_all, preferred_element_type=jnp.float32)
    starts = [((-e) % n_row) * width for e in range(n_row)]
    return [numer_h_all[:, s:s + width] for s in starts], numer_w


def slot_terms(values, lists, counts, w_tile, h_stack, row_index):
    row_blocks, stored, width = values.shape[0], values.shape[1], values.shape[2]
    n_row, rank = h_stack.shape[0], h_stack.shape[1]
    tile_rows = w_tile.shape[0]
    w_rows = w_tile.reshape(row_blocks, width, rank)
    numer_h_stack = jnp.zeros((n_row, rank, width), jnp.float32)
    parts_w = []
    for brow in range(row_blocks):
        part_w = jnp.zeros((width, rank), jnp.float32)
        for slot in range(stored):
            target = lists[brow, slot]
            live = slot < counts[brow]
            h_block = lax.dynamic_index_in_dim(
                h_stack, (row_index - target) % n_row, 0, keepdims=False
            )
            product = jnp.dot(w_rows[brow], h_block, preferred_element_type=jnp.float32)
            ratios = (values[brow, slot].astype(jnp.float32) / product).astype(jnp.bfloat16)
            ratios = jnp.where(live, ratios, jnp.zeros_like(ratios))
            part_h = jnp.einsum(
                "ik,ij->kj", w_rows[brow], ratios, preferred_element_type=jnp.float32
            )
            part_w = part_w + jnp.einsum(
                "ij,kj->ik", ratios, h_block, preferred_element_type=jnp.float32
            )
            offset = (target - row_index) % n_row
            old = lax.dynamic_index_in_dim(numer_h_stack, offset, 0, keepdims=True)
            numer_h_stack = lax.dynamic_update_index_in_dim(
                numer_h_stack, old + part_h[None], offset, 0
            )
        parts_w.append(part_w)
    numer_w = jnp.stack(parts_w).reshape(tile_rows, rank)
    return [numer_h_stack[e] for e in range(n_row)], numer_w


def body(a_blocks, block_list, block_count, w_factor, h_factor):
    values = a_blocks[0, 0]
    lists = block_list[0, 0]
    counts = block_count[0, 0]
    w_tile = w_factor[0]
    row_blocks, stored, width = values.shape[0], values.shape[1], values.shape[2]
    rank = w_tile.shape[1]
    tile_rows = w_tile.shape[0]
    n_row = lax.axis_size("row")
    n_col = lax.axis_size("col")
    n_sub = lax.axis_size("sub")
    row_index = lax.axis_index("row")
    col_index = lax.axis_index("col")

    sub_index = lax.axis_index("sub")
    half = width // n_sub
    own_piece = lax.dynamic_slice_in_dim(h_factor, sub_index * half, half, 1)
    w_sum = jnp.sum(w_tile.astype(jnp.float32), axis=0)
    middle = n_row // 2
    later, _ = lax.optimization_barrier((own_piece, w_sum))
    arrived = {
        d: shifted(own_piece if d == middle else later, "row", d) for d in range(1, n_row)
    }
    fetched = jnp.stack([arrived[d] for d in range(1, n_row)])
    swapped = [fetched] + [shifted(fetched, "sub", k) for k in range(1, n_sub)]
    others = assemble(swapped, sub_index, n_sub, 2)
    h_stack = jnp.concatenate([h_factor[None], others])
    h_sum = jnp.sum(h_stack.astype(jnp.float32), axis=(0, 2))

    if tile_rows * n_row * width * 4 <= (8 << 20):
        numer_h_stack, numer_w = dense_terms(values, lists, counts, w_tile, h_stack, row_index)
    else:
        numer_h_stack, numer_w = slot_terms(values, lists, counts, w_tile, h_stack, row_index)

    share = tile_rows // n_col
    chunks = numer_w.reshape(n_col, share, rank)
    h_rows = as_rows(h_sum, rank)
    mine_w = lax.dynamic_index_in_dim(chunks, col_index, 0, keepdims=False)
    got_h = h_rows
    for d in range(1, n_col):
        chunk = lax.dynamic_index_in_dim(chunks, (col_index + d) % n_col, 0, keepdims=False)
        message = shifted(jnp.concatenate([chunk, h_rows]), "col", d)
        mine_w = mine_w + message[:share]
        got_h = got_h + message[share:]
    h_total = from_rows(got_h, rank)

    w_rows_sum = as_rows(w_sum, width)
    messages = [
        jnp.concatenate([x[:, p * half:(p + 1) * half] for x in numer_h_stack + [w_rows_sum]])
        for p in range(n_sub)
    ]
    def piece_message(k):
        want = (sub_index + k) % n_sub
        chosen = messages[0]
        for p in range(1, n_sub):
            chosen = jnp.where(want == p, messages[p], chosen)
        return chosen
    reduced = piece_message(0)
    for k in range(1, n_sub):
        reduced = reduced + shifted(piece_message(k), "sub", k)
    extra = reduced[n_row * rank:]
    mine_h = reduced[:rank]
    got_w = extra
    for d in reversed(range(1, n_row)):
        message = shifted(jnp.concatenate([reduced[d * rank:(d + 1) * rank], extra]), "row", d)
        mine_h = mine_h + message[:rank]
        got_w = got_w + message[rank:]
    final = jnp.concatenate([mine_h, got_w])
    total = assemble([final] + [shifted(final, "sub", k) for k in range(1, n_sub)], sub_index, n_sub, 1)
    numer_h = total[:rank]
    w_total = from_rows(total[rank:], rank)

    h_new = h_factor.astype(jnp.float32) * numer_h / w_total[:, None]
    w_part = lax.dynamic_slice_in_dim(w_tile, col_index * share, share, 0).astype(jnp.float32)
    w_new = (w_part * mine_w / h_total[None, :])[None]
    return (w_new, h_new)


def solution(mesh):
    placed = (
        P(("grp", "row", "sub"), "col", None, None, None, None),
        P(("grp", "row", "sub"), "col", None, None),
        P(("grp", "row", "sub"), "col", None),
        P(("grp", "row", "sub"), None, None),
        P(None, ("grp", "row", "col")),
    )
    return jax.shard_map(
        body,
        mesh=mesh,
        in_specs=placed,
        out_specs=(P(("grp", "row", "sub"), "col", None), P(None, ("grp", "row", "col"))),
        check_vma=False,
    )
```

```python
import jax
import jax.numpy as jnp
from jax import lax
from jax.sharding import PartitionSpec as P


def shifted(value, axis, by):
    length = lax.axis_size(axis)
    return lax.ppermute(value, axis, [(i, (i + by) % length) for i in range(length)])


def as_rows(vector, width):
    size = vector.shape[0]
    rows = -(-size // width)
    flat = jnp.pad(vector, (0, rows * width - size)).reshape(rows, width)
    return jnp.pad(flat, ((0, (-rows) % 8), (0, 0)))


def from_rows(rows, size):
    return rows.reshape(-1)[:size]


def assemble(pieces, index, count, axis):
    out = []
    for j in range(count):
        want = (index - j) % count
        chosen = pieces[0]
        for k in range(1, count):
            chosen = jnp.where(want == k, pieces[k], chosen)
        out.append(chosen)
    return jnp.concatenate(out, axis=axis)


def dense_terms(values, lists, counts, w_tile, h_stack, row_index):
    row_blocks, stored, width = values.shape[0], values.shape[1], values.shape[2]
    n_row, rank = h_stack.shape[0], h_stack.shape[1]
    tile_rows = w_tile.shape[0]
    h_all = jnp.concatenate([h_stack[d] for d in range(n_row)], axis=1)
    product = jnp.dot(w_tile, h_all, preferred_element_type=jnp.float32)
    chunks = []
    for d in range(n_row):
        block = (row_index - d) % n_row
        a_d = jnp.zeros((row_blocks, width, width), values.dtype)
        covered = jnp.zeros((row_blocks,), jnp.bool_)
        for slot in range(stored):
            match = (lists[:, slot] == block) & (slot < counts)
            a_d = jnp.where(match[:, None, None], values[:, slot], a_d)
            covered = covered | match
        p_d = product[:, d * width:(d + 1) * width].reshape(row_blocks, width, width)
        r_d = jnp.where(covered[:, None, None], a_d.astype(jnp.float32) / p_d, 0.0)
        chunks.append(r_d.astype(jnp.bfloat16).reshape(tile_rows, width))
    ratios = jnp.concatenate(chunks, axis=1)
    numer_h_all = jnp.einsum("ik,ij->kj", w_tile, ratios, preferred_element_type=jnp.float32)
    numer_w = jnp.einsum("ij,kj->ik", ratios, h_all, preferred_element_type=jnp.float32)
    starts = [((-e) % n_row) * width for e in range(n_row)]
    return [numer_h_all[:, s:s + width] for s in starts], numer_w


def slot_terms(values, lists, counts, w_tile, h_stack, row_index):
    row_blocks, stored, width = values.shape[0], values.shape[1], values.shape[2]
    n_row, rank = h_stack.shape[0], h_stack.shape[1]
    tile_rows = w_tile.shape[0]
    w_rows = w_tile.reshape(row_blocks, width, rank)
    numer_h_stack = jnp.zeros((n_row, rank, width), jnp.float32)
    parts_w = []
    for brow in range(row_blocks):
        part_w = jnp.zeros((width, rank), jnp.float32)
        for slot in range(stored):
            target = lists[brow, slot]
            live = slot < counts[brow]
            h_block = lax.dynamic_index_in_dim(
                h_stack, (row_index - target) % n_row, 0, keepdims=False
            )
            product = jnp.dot(w_rows[brow], h_block, preferred_element_type=jnp.float32)
            ratios = (values[brow, slot].astype(jnp.float32) / product).astype(jnp.bfloat16)
            ratios = jnp.where(live, ratios, jnp.zeros_like(ratios))
            part_h = jnp.einsum(
                "ik,ij->kj", w_rows[brow], ratios, preferred_element_type=jnp.float32
            )
            part_w = part_w + jnp.einsum(
                "ij,kj->ik", ratios, h_block, preferred_element_type=jnp.float32
            )
            offset = (target - row_index) % n_row
            old = lax.dynamic_index_in_dim(numer_h_stack, offset, 0, keepdims=True)
            numer_h_stack = lax.dynamic_update_index_in_dim(
                numer_h_stack, old + part_h[None], offset, 0
            )
        parts_w.append(part_w)
    numer_w = jnp.stack(parts_w).reshape(tile_rows, rank)
    return [numer_h_stack[e] for e in range(n_row)], numer_w


def body(a_blocks, block_list, block_count, w_factor, h_factor):
    values = a_blocks[0, 0]
    lists = block_list[0, 0]
    counts = block_count[0, 0]
    w_tile = w_factor[0]
    row_blocks, stored, width = values.shape[0], values.shape[1], values.shape[2]
    rank = w_tile.shape[1]
    tile_rows = w_tile.shape[0]
    n_row = lax.axis_size("row")
    n_col = lax.axis_size("col")
    n_sub = lax.axis_size("sub")
    row_index = lax.axis_index("row")
    col_index = lax.axis_index("col")

    sub_index = lax.axis_index("sub")
    half = width // n_sub
    own_piece = lax.dynamic_slice_in_dim(h_factor, sub_index * half, half, 1)
    arrived = {d: shifted(own_piece, "row", d) for d in reversed(range(1, n_row))}
    fetched = jnp.stack([arrived[d] for d in range(1, n_row)])
    swapped = [fetched] + [shifted(fetched, "sub", k) for k in range(1, n_sub)]
    others = assemble(swapped, sub_index, n_sub, 2)
    h_stack = jnp.concatenate([h_factor[None], others])
    h_sum = jnp.sum(h_stack.astype(jnp.float32), axis=(0, 2))
    w_sum = jnp.sum(w_tile.astype(jnp.float32), axis=0)

    if tile_rows * n_row * width * 4 <= (8 << 20):
        numer_h_stack, numer_w = dense_terms(values, lists, counts, w_tile, h_stack, row_index)
    else:
        numer_h_stack, numer_w = slot_terms(values, lists, counts, w_tile, h_stack, row_index)

    share = tile_rows // n_col
    chunks = numer_w.reshape(n_col, share, rank)
    h_rows = as_rows(h_sum, rank)
    mine_w = lax.dynamic_index_in_dim(chunks, col_index, 0, keepdims=False)
    got_h = h_rows
    for d in range(1, n_col):
        chunk = lax.dynamic_index_in_dim(chunks, (col_index + d) % n_col, 0, keepdims=False)
        message = shifted(jnp.concatenate([chunk, h_rows]), "col", d)
        mine_w = mine_w + message[:share]
        got_h = got_h + message[share:]
    h_total = from_rows(got_h, rank)
    w_part = lax.dynamic_slice_in_dim(w_tile, col_index * share, share, 0)
    w_new = (w_part.astype(jnp.float32) * mine_w / h_total[None, :])[None]

    w_rows_sum = as_rows(w_sum, width)
    messages = [
        jnp.concatenate([x[:, p * half:(p + 1) * half] for x in numer_h_stack + [w_rows_sum]])
        for p in range(n_sub)
    ]
    def piece_message(k):
        want = (sub_index + k) % n_sub
        chosen = messages[0]
        for p in range(1, n_sub):
            chosen = jnp.where(want == p, messages[p], chosen)
        return chosen
    reduced = piece_message(0)
    for k in range(1, n_sub):
        reduced = reduced + shifted(piece_message(k), "sub", k)
    extra = reduced[n_row * rank:]
    mine_h = reduced[:rank]
    got_w = extra
    for d in reversed(range(1, n_row)):
        message = shifted(jnp.concatenate([reduced[d * rank:(d + 1) * rank], extra]), "row", d)
        if d == 1:
            message, w_new = lax.optimization_barrier((message, w_new))
        mine_h = mine_h + message[:rank]
        got_w = got_w + message[rank:]
    final = jnp.concatenate([mine_h, got_w])
    total = assemble([final] + [shifted(final, "sub", k) for k in range(1, n_sub)], sub_index, n_sub, 1)
    numer_h = total[:rank]
    w_total = from_rows(total[rank:], rank)

    h_new = h_factor.astype(jnp.float32) * numer_h / w_total[:, None]
    return (w_new, h_new)


def solution(mesh):
    placed = (
        P(("grp", "row", "sub"), "col", None, None, None, None),
        P(("grp", "row", "sub"), "col", None, None),
        P(("grp", "row", "sub"), "col", None),
        P(("grp", "row", "sub"), None, None),
        P(None, ("grp", "row", "col")),
    )
    return jax.shard_map(
        body,
        mesh=mesh,
        in_specs=placed,
        out_specs=(P(("grp", "row", "sub"), "col", None), P(None, ("grp", "row", "col"))),
        check_vma=False,
    )
```

```python
import jax
import jax.numpy as jnp
from jax import lax
from jax.sharding import PartitionSpec as P


def shifted(value, axis, by):
    length = lax.axis_size(axis)
    return lax.ppermute(value, axis, [(i, (i + by) % length) for i in range(length)])


def as_rows(vector, width):
    size = vector.shape[0]
    rows = -(-size // width)
    flat = jnp.pad(vector, (0, rows * width - size)).reshape(rows, width)
    return jnp.pad(flat, ((0, (-rows) % 8), (0, 0)))


def from_rows(rows, size):
    return rows.reshape(-1)[:size]


def assemble(pieces, index, count, axis):
    out = []
    for j in range(count):
        want = (index - j) % count
        chosen = pieces[0]
        for k in range(1, count):
            chosen = jnp.where(want == k, pieces[k], chosen)
        out.append(chosen)
    return jnp.concatenate(out, axis=axis)


def dense_terms(values, lists, counts, w_tile, h_stack, row_index):
    row_blocks, stored, width = values.shape[0], values.shape[1], values.shape[2]
    n_row, rank = h_stack.shape[0], h_stack.shape[1]
    tile_rows = w_tile.shape[0]
    h_rest = jnp.concatenate([h_stack[d] for d in range(1, n_row)], axis=1)
    product = jnp.concatenate(
        [
            jnp.dot(w_tile, h_stack[0], preferred_element_type=jnp.float32),
            jnp.dot(w_tile, h_rest, preferred_element_type=jnp.float32),
        ],
        axis=1,
    )
    chunks = []
    for d in range(n_row):
        block = (row_index - d) % n_row
        a_d = jnp.zeros((row_blocks, width, width), values.dtype)
        covered = jnp.zeros((row_blocks,), jnp.bool_)
        for slot in range(stored):
            match = (lists[:, slot] == block) & (slot < counts)
            a_d = jnp.where(match[:, None, None], values[:, slot], a_d)
            covered = covered | match
        p_d = product[:, d * width:(d + 1) * width].reshape(row_blocks, width, width)
        r_d = jnp.where(covered[:, None, None], a_d.astype(jnp.float32) / p_d, 0.0)
        chunks.append(r_d.astype(jnp.bfloat16).reshape(tile_rows, width))
    ratios_rest = jnp.concatenate(chunks[1:], axis=1)
    numer_h_all = jnp.concatenate(
        [
            jnp.einsum("ik,ij->kj", w_tile, chunks[0], preferred_element_type=jnp.float32),
            jnp.einsum("ik,ij->kj", w_tile, ratios_rest, preferred_element_type=jnp.float32),
        ],
        axis=1,
    )
    numer_w = jnp.einsum(
        "ij,kj->ik", chunks[0], h_stack[0], preferred_element_type=jnp.float32
    ) + jnp.einsum("ij,kj->ik", ratios_rest, h_rest, preferred_element_type=jnp.float32)
    starts = [((-e) % n_row) * width for e in range(n_row)]
    return [numer_h_all[:, s:s + width] for s in starts], numer_w


def slot_terms(values, lists, counts, w_tile, h_stack, row_index):
    row_blocks, stored, width = values.shape[0], values.shape[1], values.shape[2]
    n_row, rank = h_stack.shape[0], h_stack.shape[1]
    tile_rows = w_tile.shape[0]
    w_rows = w_tile.reshape(row_blocks, width, rank)
    numer_h_stack = jnp.zeros((n_row, rank, width), jnp.float32)
    parts_w = []
    for brow in range(row_blocks):
        part_w = jnp.zeros((width, rank), jnp.float32)
        for slot in range(stored):
            target = lists[brow, slot]
            live = slot < counts[brow]
            h_block = lax.dynamic_index_in_dim(
                h_stack, (row_index - target) % n_row, 0, keepdims=False
            )
            product = jnp.dot(w_rows[brow], h_block, preferred_element_type=jnp.float32)
            ratios = (values[brow, slot].astype(jnp.float32) / product).astype(jnp.bfloat16)
            ratios = jnp.where(live, ratios, jnp.zeros_like(ratios))
            part_h = jnp.einsum(
                "ik,ij->kj", w_rows[brow], ratios, preferred_element_type=jnp.float32
            )
            part_w = part_w + jnp.einsum(
                "ij,kj->ik", ratios, h_block, preferred_element_type=jnp.float32
            )
            offset = (target - row_index) % n_row
            old = lax.dynamic_index_in_dim(numer_h_stack, offset, 0, keepdims=True)
            numer_h_stack = lax.dynamic_update_index_in_dim(
                numer_h_stack, old + part_h[None], offset, 0
            )
        parts_w.append(part_w)
    numer_w = jnp.stack(parts_w).reshape(tile_rows, rank)
    return [numer_h_stack[e] for e in range(n_row)], numer_w


def body(a_blocks, block_list, block_count, w_factor, h_factor):
    values = a_blocks[0, 0]
    lists = block_list[0, 0]
    counts = block_count[0, 0]
    w_tile = w_factor[0]
    row_blocks, stored, width = values.shape[0], values.shape[1], values.shape[2]
    rank = w_tile.shape[1]
    tile_rows = w_tile.shape[0]
    n_row = lax.axis_size("row")
    n_col = lax.axis_size("col")
    n_sub = lax.axis_size("sub")
    row_index = lax.axis_index("row")
    col_index = lax.axis_index("col")

    sub_index = lax.axis_index("sub")
    half = width // n_sub
    own_piece = lax.dynamic_slice_in_dim(h_factor, sub_index * half, half, 1)
    arrived = {d: shifted(own_piece, "row", d) for d in reversed(range(1, n_row))}
    fetched = jnp.stack([arrived[d] for d in range(1, n_row)])
    swapped = [fetched] + [shifted(fetched, "sub", k) for k in range(1, n_sub)]
    others = assemble(swapped, sub_index, n_sub, 2)
    h_stack = jnp.concatenate([h_factor[None], others])
    h_sum = jnp.sum(h_stack.astype(jnp.float32), axis=(0, 2))
    w_sum = jnp.sum(w_tile.astype(jnp.float32), axis=0)

    if tile_rows * n_row * width * 4 <= (8 << 20):
        numer_h_stack, numer_w = dense_terms(values, lists, counts, w_tile, h_stack, row_index)
    else:
        numer_h_stack, numer_w = slot_terms(values, lists, counts, w_tile, h_stack, row_index)

    share = tile_rows // n_col
    chunks = numer_w.reshape(n_col, share, rank)
    h_rows = as_rows(h_sum, rank)
    mine_w = lax.dynamic_index_in_dim(chunks, col_index, 0, keepdims=False)
    got_h = h_rows
    for d in range(1, n_col):
        chunk = lax.dynamic_index_in_dim(chunks, (col_index + d) % n_col, 0, keepdims=False)
        message = shifted(jnp.concatenate([chunk, h_rows]), "col", d)
        mine_w = mine_w + message[:share]
        got_h = got_h + message[share:]
    h_total = from_rows(got_h, rank)

    w_rows_sum = as_rows(w_sum, width)
    messages = [
        jnp.concatenate([x[:, p * half:(p + 1) * half] for x in numer_h_stack + [w_rows_sum]])
        for p in range(n_sub)
    ]
    def piece_message(k):
        want = (sub_index + k) % n_sub
        chosen = messages[0]
        for p in range(1, n_sub):
            chosen = jnp.where(want == p, messages[p], chosen)
        return chosen
    reduced = piece_message(0)
    for k in range(1, n_sub):
        reduced = reduced + shifted(piece_message(k), "sub", k)
    extra = reduced[n_row * rank:]
    mine_h = reduced[:rank]
    got_w = extra
    for d in reversed(range(1, n_row)):
        message = shifted(jnp.concatenate([reduced[d * rank:(d + 1) * rank], extra]), "row", d)
        mine_h = mine_h + message[:rank]
        got_w = got_w + message[rank:]
    final = jnp.concatenate([mine_h, got_w])
    total = assemble([final] + [shifted(final, "sub", k) for k in range(1, n_sub)], sub_index, n_sub, 1)
    numer_h = total[:rank]
    w_total = from_rows(total[rank:], rank)

    h_new = h_factor.astype(jnp.float32) * numer_h / w_total[:, None]
    w_part = lax.dynamic_slice_in_dim(w_tile, col_index * share, share, 0).astype(jnp.float32)
    w_new = (w_part * mine_w / h_total[None, :])[None]
    return (w_new, h_new)


def solution(mesh):
    placed = (
        P(("grp", "row", "sub"), "col", None, None, None, None),
        P(("grp", "row", "sub"), "col", None, None),
        P(("grp", "row", "sub"), "col", None),
        P(("grp", "row", "sub"), None, None),
        P(None, ("grp", "row", "col")),
    )
    return jax.shard_map(
        body,
        mesh=mesh,
        in_specs=placed,
        out_specs=(P(("grp", "row", "sub"), "col", None), P(None, ("grp", "row", "col"))),
        check_vma=False,
    )
```

```python
import jax
import jax.numpy as jnp
from jax import lax
from jax.sharding import PartitionSpec as P


def shifted(value, axis, by):
    length = lax.axis_size(axis)
    return lax.ppermute(value, axis, [(i, (i + by) % length) for i in range(length)])


def as_rows(vector, width):
    size = vector.shape[0]
    rows = -(-size // width)
    flat = jnp.pad(vector, (0, rows * width - size)).reshape(rows, width)
    return jnp.pad(flat, ((0, (-rows) % 8), (0, 0)))


def from_rows(rows, size):
    return rows.reshape(-1)[:size]


def assemble(pieces, index, count, axis):
    out = []
    for j in range(count):
        want = (index - j) % count
        chosen = pieces[0]
        for k in range(1, count):
            chosen = jnp.where(want == k, pieces[k], chosen)
        out.append(chosen)
    return jnp.concatenate(out, axis=axis)


def dense_terms(values, lists, counts, w_tile, h_stack, row_index):
    row_blocks, stored, width = values.shape[0], values.shape[1], values.shape[2]
    n_row, rank = h_stack.shape[0], h_stack.shape[1]
    tile_rows = w_tile.shape[0]
    h_rest = jnp.concatenate([h_stack[d] for d in range(1, n_row)], axis=1)
    product = jnp.concatenate(
        [
            jnp.dot(w_tile, h_stack[0], preferred_element_type=jnp.float32),
            jnp.dot(w_tile, h_rest, preferred_element_type=jnp.float32),
        ],
        axis=1,
    )
    chunks = []
    for d in range(n_row):
        block = (row_index - d) % n_row
        a_d = jnp.zeros((row_blocks, width, width), values.dtype)
        covered = jnp.zeros((row_blocks,), jnp.bool_)
        for slot in range(stored):
            match = (lists[:, slot] == block) & (slot < counts)
            a_d = jnp.where(match[:, None, None], values[:, slot], a_d)
            covered = covered | match
        p_d = product[:, d * width:(d + 1) * width].reshape(row_blocks, width, width)
        r_d = jnp.where(covered[:, None, None], a_d.astype(jnp.float32) / p_d, 0.0)
        chunks.append(r_d.astype(jnp.bfloat16).reshape(tile_rows, width))
    ratios_rest = jnp.concatenate(chunks[1:], axis=1)
    numer_h_all = jnp.concatenate(
        [
            jnp.einsum("ik,ij->kj", w_tile, chunks[0], preferred_element_type=jnp.float32),
            jnp.einsum("ik,ij->kj", w_tile, ratios_rest, preferred_element_type=jnp.float32),
        ],
        axis=1,
    )
    numer_w = jnp.einsum(
        "ij,kj->ik", chunks[0], h_stack[0], preferred_element_type=jnp.float32
    ) + jnp.einsum("ij,kj->ik", ratios_rest, h_rest, preferred_element_type=jnp.float32)
    starts = [((-e) % n_row) * width for e in range(n_row)]
    return [numer_h_all[:, s:s + width] for s in starts], numer_w


def slot_terms(values, lists, counts, w_tile, h_stack, row_index):
    row_blocks, stored, width = values.shape[0], values.shape[1], values.shape[2]
    n_row, rank = h_stack.shape[0], h_stack.shape[1]
    tile_rows = w_tile.shape[0]
    w_rows = w_tile.reshape(row_blocks, width, rank)
    numer_h_stack = jnp.zeros((n_row, rank, width), jnp.float32)
    parts_w = []
    for brow in range(row_blocks):
        part_w = jnp.zeros((width, rank), jnp.float32)
        for slot in range(stored):
            target = lists[brow, slot]
            live = slot < counts[brow]
            h_block = lax.dynamic_index_in_dim(
                h_stack, (row_index - target) % n_row, 0, keepdims=False
            )
            product = jnp.dot(w_rows[brow], h_block, preferred_element_type=jnp.float32)
            ratios = (values[brow, slot].astype(jnp.float32) / product).astype(jnp.bfloat16)
            ratios = jnp.where(live, ratios, jnp.zeros_like(ratios))
            part_h = jnp.einsum(
                "ik,ij->kj", w_rows[brow], ratios, preferred_element_type=jnp.float32
            )
            part_w = part_w + jnp.einsum(
                "ij,kj->ik", ratios, h_block, preferred_element_type=jnp.float32
            )
            offset = (target - row_index) % n_row
            old = lax.dynamic_index_in_dim(numer_h_stack, offset, 0, keepdims=True)
            numer_h_stack = lax.dynamic_update_index_in_dim(
                numer_h_stack, old + part_h[None], offset, 0
            )
        parts_w.append(part_w)
    numer_w = jnp.stack(parts_w).reshape(tile_rows, rank)
    return [numer_h_stack[e] for e in range(n_row)], numer_w


def body(a_blocks, block_list, block_count, w_factor, h_factor):
    values = a_blocks[0, 0]
    lists = block_list[0, 0]
    counts = block_count[0, 0]
    w_tile = w_factor[0]
    row_blocks, stored, width = values.shape[0], values.shape[1], values.shape[2]
    rank = w_tile.shape[1]
    tile_rows = w_tile.shape[0]
    n_row = lax.axis_size("row")
    n_col = lax.axis_size("col")
    n_sub = lax.axis_size("sub")
    row_index = lax.axis_index("row")
    col_index = lax.axis_index("col")

    sub_index = lax.axis_index("sub")
    half = width // n_sub
    own_piece = lax.dynamic_slice_in_dim(h_factor, sub_index * half, half, 1)
    arrived = {d: shifted(own_piece, "row", d) for d in reversed(range(1, n_row))}
    fetched = jnp.stack([arrived[d] for d in range(1, n_row)])
    swapped = [fetched] + [shifted(fetched, "sub", k) for k in range(1, n_sub)]
    others = assemble(swapped, sub_index, n_sub, 2)
    h_stack = jnp.concatenate([h_factor[None], others])
    h_sum = jnp.sum(h_stack.astype(jnp.float32), axis=(0, 2))
    w_sum = jnp.sum(w_tile.astype(jnp.float32), axis=0)

    if tile_rows * n_row * width * 4 <= (8 << 20):
        numer_h_stack, numer_w = dense_terms(values, lists, counts, w_tile, h_stack, row_index)
    else:
        numer_h_stack, numer_w = slot_terms(values, lists, counts, w_tile, h_stack, row_index)

    share = tile_rows // n_col
    chunks = numer_w.reshape(n_col, share, rank)
    h_rows = as_rows(h_sum, rank)
    mine_w = lax.dynamic_index_in_dim(chunks, col_index, 0, keepdims=False)
    got_h = h_rows
    for d in range(1, n_col):
        chunk = lax.dynamic_index_in_dim(chunks, (col_index + d) % n_col, 0, keepdims=False)
        message = shifted(jnp.concatenate([chunk, h_rows]), "col", d)
        mine_w = mine_w + message[:share]
        got_h = got_h + message[share:]
    h_total = from_rows(got_h, rank)
    w_part = lax.dynamic_slice_in_dim(w_tile, col_index * share, share, 0)
    w_new = (w_part.astype(jnp.float32) * mine_w / h_total[None, :])[None]

    w_rows_sum = as_rows(w_sum, width)
    messages = [
        jnp.concatenate([x[:, p * half:(p + 1) * half] for x in numer_h_stack + [w_rows_sum]])
        for p in range(n_sub)
    ]
    def piece_message(k):
        want = (sub_index + k) % n_sub
        chosen = messages[0]
        for p in range(1, n_sub):
            chosen = jnp.where(want == p, messages[p], chosen)
        return chosen
    reduced = piece_message(0)
    for k in range(1, n_sub):
        reduced = reduced + shifted(piece_message(k), "sub", k)
    extra = reduced[n_row * rank:]
    mine_h = reduced[:rank]
    got_w = extra
    for d in reversed(range(1, n_row)):
        message = shifted(jnp.concatenate([reduced[d * rank:(d + 1) * rank], extra]), "row", d)
        if d == 1:
            message, w_new = lax.optimization_barrier((message, w_new))
        mine_h = mine_h + message[:rank]
        got_w = got_w + message[rank:]
    final = jnp.concatenate([mine_h, got_w])
    total = assemble([final] + [shifted(final, "sub", k) for k in range(1, n_sub)], sub_index, n_sub, 1)
    numer_h = total[:rank]
    w_total = from_rows(total[rank:], rank)

    h_new = h_factor.astype(jnp.float32) * numer_h / w_total[:, None]
    return (w_new, h_new)


def solution(mesh):
    placed = (
        P(("grp", "row", "sub"), "col", None, None, None, None),
        P(("grp", "row", "sub"), "col", None, None),
        P(("grp", "row", "sub"), "col", None),
        P(("grp", "row", "sub"), None, None),
        P(None, ("grp", "row", "col")),
    )
    return jax.shard_map(
        body,
        mesh=mesh,
        in_specs=placed,
        out_specs=(P(("grp", "row", "sub"), "col", None), P(None, ("grp", "row", "col"))),
        check_vma=False,
    )
```

```python
import jax
import jax.numpy as jnp
from jax import lax
from jax.sharding import PartitionSpec as P


def shifted(value, axis, by):
    length = lax.axis_size(axis)
    return lax.ppermute(value, axis, [(i, (i + by) % length) for i in range(length)])


def as_rows(vector, width):
    size = vector.shape[0]
    rows = -(-size // width)
    flat = jnp.pad(vector, (0, rows * width - size)).reshape(rows, width)
    return jnp.pad(flat, ((0, (-rows) % 8), (0, 0)))


def from_rows(rows, size):
    return rows.reshape(-1)[:size]


def assemble(pieces, index, count, axis):
    out = []
    for j in range(count):
        want = (index - j) % count
        chosen = pieces[0]
        for k in range(1, count):
            chosen = jnp.where(want == k, pieces[k], chosen)
        out.append(chosen)
    return jnp.concatenate(out, axis=axis)


def dense_terms(values, lists, counts, w_tile, h_stack, row_index):
    row_blocks, stored, width = values.shape[0], values.shape[1], values.shape[2]
    n_row, rank = h_stack.shape[0], h_stack.shape[1]
    tile_rows = w_tile.shape[0]
    h_rest = jnp.concatenate([h_stack[d] for d in range(1, n_row)], axis=1)
    product = jnp.concatenate(
        [
            jnp.dot(w_tile, h_stack[0], preferred_element_type=jnp.float32),
            jnp.dot(w_tile, h_rest, preferred_element_type=jnp.float32),
        ],
        axis=1,
    )
    chunks = []
    for d in range(n_row):
        block = (row_index - d) % n_row
        a_d = jnp.zeros((row_blocks, width, width), values.dtype)
        covered = jnp.zeros((row_blocks,), jnp.bool_)
        for slot in range(stored):
            match = (lists[:, slot] == block) & (slot < counts)
            a_d = jnp.where(match[:, None, None], values[:, slot], a_d)
            covered = covered | match
        p_d = product[:, d * width:(d + 1) * width].reshape(row_blocks, width, width)
        r_d = jnp.where(covered[:, None, None], a_d.astype(jnp.float32) / p_d, 0.0)
        chunks.append(r_d.astype(jnp.bfloat16).reshape(tile_rows, width))
    ratios_rest = jnp.concatenate(chunks[1:], axis=1)
    numer_h_all = jnp.concatenate(
        [
            jnp.einsum("ik,ij->kj", w_tile, chunks[0], preferred_element_type=jnp.float32),
            jnp.einsum("ik,ij->kj", w_tile, ratios_rest, preferred_element_type=jnp.float32),
        ],
        axis=1,
    )
    numer_w = jnp.einsum(
        "ij,kj->ik", chunks[0], h_stack[0], preferred_element_type=jnp.float32
    ) + jnp.einsum("ij,kj->ik", ratios_rest, h_rest, preferred_element_type=jnp.float32)
    starts = [((-e) % n_row) * width for e in range(n_row)]
    return [numer_h_all[:, s:s + width] for s in starts], numer_w


def slot_terms(values, lists, counts, w_tile, h_stack, row_index):
    row_blocks, stored, width = values.shape[0], values.shape[1], values.shape[2]
    n_row, rank = h_stack.shape[0], h_stack.shape[1]
    tile_rows = w_tile.shape[0]
    w_rows = w_tile.reshape(row_blocks, width, rank)
    numer_h_stack = jnp.zeros((n_row, rank, width), jnp.float32)
    parts_w = []
    for brow in range(row_blocks):
        part_w = jnp.zeros((width, rank), jnp.float32)
        for slot in range(stored):
            target = lists[brow, slot]
            live = slot < counts[brow]
            h_block = lax.dynamic_index_in_dim(
                h_stack, (row_index - target) % n_row, 0, keepdims=False
            )
            product = jnp.dot(w_rows[brow], h_block, preferred_element_type=jnp.float32)
            ratios = (values[brow, slot].astype(jnp.float32) / product).astype(jnp.bfloat16)
            ratios = jnp.where(live, ratios, jnp.zeros_like(ratios))
            part_h = jnp.einsum(
                "ik,ij->kj", w_rows[brow], ratios, preferred_element_type=jnp.float32
            )
            part_w = part_w + jnp.einsum(
                "ij,kj->ik", ratios, h_block, preferred_element_type=jnp.float32
            )
            offset = (target - row_index) % n_row
            old = lax.dynamic_index_in_dim(numer_h_stack, offset, 0, keepdims=True)
            numer_h_stack = lax.dynamic_update_index_in_dim(
                numer_h_stack, old + part_h[None], offset, 0
            )
        parts_w.append(part_w)
    numer_w = jnp.stack(parts_w).reshape(tile_rows, rank)
    return [numer_h_stack[e] for e in range(n_row)], numer_w


def piece_body(values, lists, counts, w_tile, h_factor):
    row_blocks, stored, width = values.shape[0], values.shape[1], values.shape[2]
    rank = w_tile.shape[1]
    tile_rows = w_tile.shape[0]
    n_row = lax.axis_size("row")
    n_col = lax.axis_size("col")
    n_sub = lax.axis_size("sub")
    row_index = lax.axis_index("row")
    col_index = lax.axis_index("col")
    sub_index = lax.axis_index("sub")
    half = width // n_sub

    own_piece = lax.dynamic_slice_in_dim(h_factor, sub_index * half, half, 1)
    h_pieces = [own_piece] + [shifted(own_piece, "row", d) for d in range(1, n_row)]
    h_cols = jnp.concatenate(h_pieces, axis=1)

    tiles = [(w_tile, lax.dynamic_slice_in_dim(values, sub_index * half, half, 3), lists, counts)]
    for k in range(1, n_sub):
        piece = lax.dynamic_slice_in_dim(values, ((sub_index + k) % n_sub) * half, half, 3)
        tiles.append(tuple(shifted(x, "sub", k) for x in (w_tile, piece, lists, counts)))

    numer_h_piece = None
    partials_w = []
    w_chip = None
    for w_k, values_k, lists_k, counts_k in tiles:
        product = jnp.dot(w_k, h_cols, preferred_element_type=jnp.float32)
        columns = []
        for d in range(n_row):
            block = (row_index - d) % n_row
            a_d = jnp.zeros((row_blocks, width, half), values_k.dtype)
            covered = jnp.zeros((row_blocks,), jnp.bool_)
            for slot in range(stored):
                match = (lists_k[:, slot] == block) & (slot < counts_k)
                a_d = jnp.where(match[:, None, None], values_k[:, slot], a_d)
                covered = covered | match
            p_d = product[:, d * half:(d + 1) * half].reshape(row_blocks, width, half)
            r_d = jnp.where(covered[:, None, None], a_d.astype(jnp.float32) / p_d, 0.0)
            columns.append(r_d.astype(jnp.bfloat16).reshape(tile_rows, half))
        ratios = jnp.concatenate(columns, axis=1)
        part_h = jnp.einsum("ik,ij->kj", w_k, ratios, preferred_element_type=jnp.float32)
        numer_h_piece = part_h if numer_h_piece is None else numer_h_piece + part_h
        partials_w.append(jnp.einsum("ij,kj->ik", ratios, h_cols, preferred_element_type=jnp.float32))
        w_k_sum = jnp.sum(w_k.astype(jnp.float32), axis=0)
        w_chip = w_k_sum if w_chip is None else w_chip + w_k_sum

    h_part = as_rows(jnp.sum(h_cols.astype(jnp.float32), axis=1), rank)
    numer_w = partials_w[0]
    h_group = h_part
    for k in range(1, n_sub):
        back = shifted(jnp.concatenate([partials_w[k], h_part]), "sub", n_sub - k)
        numer_w = numer_w + back[:tile_rows]
        h_group = h_group + back[tile_rows:]

    share = tile_rows // n_col
    chunks = numer_w.reshape(n_col, share, rank)
    mine_w = lax.dynamic_index_in_dim(chunks, col_index, 0, keepdims=False)
    got_h = h_group
    for d in range(1, n_col):
        chunk = lax.dynamic_index_in_dim(chunks, (col_index + d) % n_col, 0, keepdims=False)
        message = shifted(jnp.concatenate([chunk, h_group]), "col", d)
        mine_w = mine_w + message[:share]
        got_h = got_h + message[share:]
    h_total = from_rows(got_h, rank)

    w_rows_sum = lax.dynamic_slice_in_dim(as_rows(w_chip, width), sub_index * half, half, 1)
    mine_h = numer_h_piece[:, :half]
    got_w = w_rows_sum
    for e in reversed(range(1, n_row)):
        d = (-e) % n_row
        message = jnp.concatenate([numer_h_piece[:, d * half:(d + 1) * half], w_rows_sum])
        message = shifted(message, "row", e)
        mine_h = mine_h + message[:rank]
        got_w = got_w + message[rank:]
    final = jnp.concatenate([mine_h, got_w])
    total = assemble([final] + [shifted(final, "sub", k) for k in range(1, n_sub)], sub_index, n_sub, 1)
    numer_h = total[:rank]
    w_total = from_rows(total[rank:], rank)

    h_new = h_factor.astype(jnp.float32) * numer_h / w_total[:, None]
    w_part = lax.dynamic_slice_in_dim(w_tile, col_index * share, share, 0).astype(jnp.float32)
    w_new = (w_part * mine_w / h_total[None, :])[None]
    return (w_new, h_new)


def body(a_blocks, block_list, block_count, w_factor, h_factor):
    values = a_blocks[0, 0]
    lists = block_list[0, 0]
    counts = block_count[0, 0]
    w_tile = w_factor[0]
    row_blocks, stored, width = values.shape[0], values.shape[1], values.shape[2]
    rank = w_tile.shape[1]
    tile_rows = w_tile.shape[0]
    n_row = lax.axis_size("row")
    n_col = lax.axis_size("col")
    n_sub = lax.axis_size("sub")
    row_index = lax.axis_index("row")
    col_index = lax.axis_index("col")

    if tile_rows * n_row * width * 4 <= (8 << 20):
        return piece_body(values, lists, counts, w_tile, h_factor)
    sub_index = lax.axis_index("sub")
    half = width // n_sub
    own_piece = lax.dynamic_slice_in_dim(h_factor, sub_index * half, half, 1)
    arrived = {d: shifted(own_piece, "row", d) for d in reversed(range(1, n_row))}
    fetched = jnp.stack([arrived[d] for d in range(1, n_row)])
    swapped = [fetched] + [shifted(fetched, "sub", k) for k in range(1, n_sub)]
    others = assemble(swapped, sub_index, n_sub, 2)
    h_stack = jnp.concatenate([h_factor[None], others])
    h_sum = jnp.sum(h_stack.astype(jnp.float32), axis=(0, 2))
    w_sum = jnp.sum(w_tile.astype(jnp.float32), axis=0)

    if tile_rows * n_row * width * 4 <= (8 << 20):
        numer_h_stack, numer_w = dense_terms(values, lists, counts, w_tile, h_stack, row_index)
    else:
        numer_h_stack, numer_w = slot_terms(values, lists, counts, w_tile, h_stack, row_index)

    share = tile_rows // n_col
    chunks = numer_w.reshape(n_col, share, rank)
    h_rows = as_rows(h_sum, rank)
    mine_w = lax.dynamic_index_in_dim(chunks, col_index, 0, keepdims=False)
    got_h = h_rows
    for d in range(1, n_col):
        chunk = lax.dynamic_index_in_dim(chunks, (col_index + d) % n_col, 0, keepdims=False)
        message = shifted(jnp.concatenate([chunk, h_rows]), "col", d)
        mine_w = mine_w + message[:share]
        got_h = got_h + message[share:]
    h_total = from_rows(got_h, rank)

    w_rows_sum = as_rows(w_sum, width)
    messages = [
        jnp.concatenate([x[:, p * half:(p + 1) * half] for x in numer_h_stack + [w_rows_sum]])
        for p in range(n_sub)
    ]
    def piece_message(k):
        want = (sub_index + k) % n_sub
        chosen = messages[0]
        for p in range(1, n_sub):
            chosen = jnp.where(want == p, messages[p], chosen)
        return chosen
    reduced = piece_message(0)
    for k in range(1, n_sub):
        reduced = reduced + shifted(piece_message(k), "sub", k)
    extra = reduced[n_row * rank:]
    mine_h = reduced[:rank]
    got_w = extra
    for d in reversed(range(1, n_row)):
        message = shifted(jnp.concatenate([reduced[d * rank:(d + 1) * rank], extra]), "row", d)
        mine_h = mine_h + message[:rank]
        got_w = got_w + message[rank:]
    final = jnp.concatenate([mine_h, got_w])
    total = assemble([final] + [shifted(final, "sub", k) for k in range(1, n_sub)], sub_index, n_sub, 1)
    numer_h = total[:rank]
    w_total = from_rows(total[rank:], rank)

    h_new = h_factor.astype(jnp.float32) * numer_h / w_total[:, None]
    w_part = lax.dynamic_slice_in_dim(w_tile, col_index * share, share, 0).astype(jnp.float32)
    w_new = (w_part * mine_w / h_total[None, :])[None]
    return (w_new, h_new)


def solution(mesh):
    placed = (
        P(("grp", "row", "sub"), "col", None, None, None, None),
        P(("grp", "row", "sub"), "col", None, None),
        P(("grp", "row", "sub"), "col", None),
        P(("grp", "row", "sub"), None, None),
        P(None, ("grp", "row", "col")),
    )
    return jax.shard_map(
        body,
        mesh=mesh,
        in_specs=placed,
        out_specs=(P(("grp", "row", "sub"), "col", None), P(None, ("grp", "row", "col"))),
        check_vma=False,
    )
```

```python
import jax
import jax.numpy as jnp
from jax import lax
from jax.sharding import PartitionSpec as P


def shifted(value, axis, by):
    length = lax.axis_size(axis)
    return lax.ppermute(value, axis, [(i, (i + by) % length) for i in range(length)])


def as_rows(vector, width):
    size = vector.shape[0]
    rows = -(-size // width)
    flat = jnp.pad(vector, (0, rows * width - size)).reshape(rows, width)
    return jnp.pad(flat, ((0, (-rows) % 8), (0, 0)))


def from_rows(rows, size):
    return rows.reshape(-1)[:size]


def assemble(pieces, index, count, axis):
    out = []
    for j in range(count):
        want = (index - j) % count
        chosen = pieces[0]
        for k in range(1, count):
            chosen = jnp.where(want == k, pieces[k], chosen)
        out.append(chosen)
    return jnp.concatenate(out, axis=axis)


def dense_terms(values, lists, counts, w_tile, h_stack, row_index):
    row_blocks, stored, width = values.shape[0], values.shape[1], values.shape[2]
    n_row, rank = h_stack.shape[0], h_stack.shape[1]
    tile_rows = w_tile.shape[0]
    h_rest = jnp.concatenate([h_stack[d] for d in range(1, n_row)], axis=1)
    product = jnp.concatenate(
        [
            jnp.dot(w_tile, h_stack[0], preferred_element_type=jnp.float32),
            jnp.dot(w_tile, h_rest, preferred_element_type=jnp.float32),
        ],
        axis=1,
    )
    chunks = []
    for d in range(n_row):
        block = (row_index - d) % n_row
        a_d = jnp.zeros((row_blocks, width, width), values.dtype)
        covered = jnp.zeros((row_blocks,), jnp.bool_)
        for slot in range(stored):
            match = (lists[:, slot] == block) & (slot < counts)
            a_d = jnp.where(match[:, None, None], values[:, slot], a_d)
            covered = covered | match
        p_d = product[:, d * width:(d + 1) * width].reshape(row_blocks, width, width)
        r_d = jnp.where(covered[:, None, None], a_d.astype(jnp.float32) / p_d, 0.0)
        chunks.append(r_d.astype(jnp.bfloat16).reshape(tile_rows, width))
    ratios_rest = jnp.concatenate(chunks[1:], axis=1)
    numer_h_all = jnp.concatenate(
        [
            jnp.einsum("ik,ij->kj", w_tile, chunks[0], preferred_element_type=jnp.float32),
            jnp.einsum("ik,ij->kj", w_tile, ratios_rest, preferred_element_type=jnp.float32),
        ],
        axis=1,
    )
    numer_w = jnp.einsum(
        "ij,kj->ik", chunks[0], h_stack[0], preferred_element_type=jnp.float32
    ) + jnp.einsum("ij,kj->ik", ratios_rest, h_rest, preferred_element_type=jnp.float32)
    starts = [((-e) % n_row) * width for e in range(n_row)]
    return [numer_h_all[:, s:s + width] for s in starts], numer_w


def slot_terms(values, lists, counts, w_tile, h_stack, row_index):
    row_blocks, stored, width = values.shape[0], values.shape[1], values.shape[2]
    n_row, rank = h_stack.shape[0], h_stack.shape[1]
    tile_rows = w_tile.shape[0]
    w_rows = w_tile.reshape(row_blocks, width, rank)
    numer_h_stack = jnp.zeros((n_row, rank, width), jnp.float32)
    parts_w = []
    for brow in range(row_blocks):
        part_w = jnp.zeros((width, rank), jnp.float32)
        for slot in range(stored):
            target = lists[brow, slot]
            live = slot < counts[brow]
            h_block = lax.dynamic_index_in_dim(
                h_stack, (row_index - target) % n_row, 0, keepdims=False
            )
            product = jnp.dot(w_rows[brow], h_block, preferred_element_type=jnp.float32)
            ratios = (values[brow, slot].astype(jnp.float32) / product).astype(jnp.bfloat16)
            ratios = jnp.where(live, ratios, jnp.zeros_like(ratios))
            part_h = jnp.einsum(
                "ik,ij->kj", w_rows[brow], ratios, preferred_element_type=jnp.float32
            )
            part_w = part_w + jnp.einsum(
                "ij,kj->ik", ratios, h_block, preferred_element_type=jnp.float32
            )
            offset = (target - row_index) % n_row
            old = lax.dynamic_index_in_dim(numer_h_stack, offset, 0, keepdims=True)
            numer_h_stack = lax.dynamic_update_index_in_dim(
                numer_h_stack, old + part_h[None], offset, 0
            )
        parts_w.append(part_w)
    numer_w = jnp.stack(parts_w).reshape(tile_rows, rank)
    return [numer_h_stack[e] for e in range(n_row)], numer_w


def piece_body(values, lists, counts, w_tile, h_factor):
    row_blocks, stored, width = values.shape[0], values.shape[1], values.shape[2]
    rank = w_tile.shape[1]
    tile_rows = w_tile.shape[0]
    n_row = lax.axis_size("row")
    n_col = lax.axis_size("col")
    n_sub = lax.axis_size("sub")
    row_index = lax.axis_index("row")
    col_index = lax.axis_index("col")
    sub_index = lax.axis_index("sub")
    half = width // n_sub

    own_piece = lax.dynamic_slice_in_dim(h_factor, sub_index * half, half, 1)
    h_pieces = [own_piece] + [shifted(own_piece, "row", d) for d in range(1, n_row)]
    h_cols = jnp.concatenate(h_pieces, axis=1)

    tiles = [(w_tile, lax.dynamic_slice_in_dim(values, sub_index * half, half, 3), lists, counts)]
    for k in range(1, n_sub):
        piece = lax.dynamic_slice_in_dim(values, ((sub_index + k) % n_sub) * half, half, 3)
        tiles.append(tuple(shifted(x, "sub", k) for x in (w_tile, piece, lists, counts)))

    numer_h_piece = None
    partials_w = []
    w_chip = None
    for w_k, values_k, lists_k, counts_k in tiles:
        product = jnp.dot(w_k, h_cols, preferred_element_type=jnp.float32)
        columns = []
        for d in range(n_row):
            block = (row_index - d) % n_row
            a_d = jnp.zeros((row_blocks, width, half), values_k.dtype)
            covered = jnp.zeros((row_blocks,), jnp.bool_)
            for slot in range(stored):
                match = (lists_k[:, slot] == block) & (slot < counts_k)
                a_d = jnp.where(match[:, None, None], values_k[:, slot], a_d)
                covered = covered | match
            p_d = product[:, d * half:(d + 1) * half].reshape(row_blocks, width, half)
            r_d = jnp.where(covered[:, None, None], a_d.astype(jnp.float32) / p_d, 0.0)
            columns.append(r_d.astype(jnp.bfloat16).reshape(tile_rows, half))
        ratios = jnp.concatenate(columns, axis=1)
        part_h = jnp.einsum("ik,ij->kj", w_k, ratios, preferred_element_type=jnp.float32)
        numer_h_piece = part_h if numer_h_piece is None else numer_h_piece + part_h
        partials_w.append(jnp.einsum("ij,kj->ik", ratios, h_cols, preferred_element_type=jnp.float32))
        w_k_sum = jnp.sum(w_k.astype(jnp.float32), axis=0)
        w_chip = w_k_sum if w_chip is None else w_chip + w_k_sum

    h_part = as_rows(jnp.sum(h_cols.astype(jnp.float32), axis=1), rank)
    numer_w = partials_w[0]
    h_group = h_part
    for k in range(1, n_sub):
        back = shifted(jnp.concatenate([partials_w[k], h_part]), "sub", n_sub - k)
        numer_w = numer_w + back[:tile_rows]
        h_group = h_group + back[tile_rows:]

    share = tile_rows // n_col
    chunks = numer_w.reshape(n_col, share, rank)
    mine_w = lax.dynamic_index_in_dim(chunks, col_index, 0, keepdims=False)
    got_h = h_group
    for d in range(1, n_col):
        chunk = lax.dynamic_index_in_dim(chunks, (col_index + d) % n_col, 0, keepdims=False)
        message = shifted(jnp.concatenate([chunk, h_group]), "col", d)
        mine_w = mine_w + message[:share]
        got_h = got_h + message[share:]

    w_rows_sum = lax.dynamic_slice_in_dim(as_rows(w_chip, width), sub_index * half, half, 1)
    mine_h = numer_h_piece[:, :half]
    got_w = w_rows_sum
    for e in reversed(range(1, n_row)):
        d = (-e) % n_row
        message = jnp.concatenate([numer_h_piece[:, d * half:(d + 1) * half], w_rows_sum])
        message = shifted(message, "row", e)
        if e == n_row - 1:
            message, mine_w, got_h = lax.optimization_barrier((message, mine_w, got_h))
        mine_h = mine_h + message[:rank]
        got_w = got_w + message[rank:]
    final = jnp.concatenate([mine_h, got_w])
    total = assemble([final] + [shifted(final, "sub", k) for k in range(1, n_sub)], sub_index, n_sub, 1)
    numer_h = total[:rank]
    w_total = from_rows(total[rank:], rank)

    h_total = from_rows(got_h, rank)
    h_new = h_factor.astype(jnp.float32) * numer_h / w_total[:, None]
    w_part = lax.dynamic_slice_in_dim(w_tile, col_index * share, share, 0).astype(jnp.float32)
    w_new = (w_part * mine_w / h_total[None, :])[None]
    return (w_new, h_new)


def body(a_blocks, block_list, block_count, w_factor, h_factor):
    values = a_blocks[0, 0]
    lists = block_list[0, 0]
    counts = block_count[0, 0]
    w_tile = w_factor[0]
    row_blocks, stored, width = values.shape[0], values.shape[1], values.shape[2]
    rank = w_tile.shape[1]
    tile_rows = w_tile.shape[0]
    n_row = lax.axis_size("row")
    n_col = lax.axis_size("col")
    n_sub = lax.axis_size("sub")
    row_index = lax.axis_index("row")
    col_index = lax.axis_index("col")

    if tile_rows * n_row * width * 4 <= (8 << 20):
        return piece_body(values, lists, counts, w_tile, h_factor)
    sub_index = lax.axis_index("sub")
    half = width // n_sub
    own_piece = lax.dynamic_slice_in_dim(h_factor, sub_index * half, half, 1)
    arrived = {d: shifted(own_piece, "row", d) for d in reversed(range(1, n_row))}
    fetched = jnp.stack([arrived[d] for d in range(1, n_row)])
    swapped = [fetched] + [shifted(fetched, "sub", k) for k in range(1, n_sub)]
    others = assemble(swapped, sub_index, n_sub, 2)
    h_stack = jnp.concatenate([h_factor[None], others])
    h_sum = jnp.sum(h_stack.astype(jnp.float32), axis=(0, 2))
    w_sum = jnp.sum(w_tile.astype(jnp.float32), axis=0)

    if tile_rows * n_row * width * 4 <= (8 << 20):
        numer_h_stack, numer_w = dense_terms(values, lists, counts, w_tile, h_stack, row_index)
    else:
        numer_h_stack, numer_w = slot_terms(values, lists, counts, w_tile, h_stack, row_index)

    share = tile_rows // n_col
    chunks = numer_w.reshape(n_col, share, rank)
    h_rows = as_rows(h_sum, rank)
    mine_w = lax.dynamic_index_in_dim(chunks, col_index, 0, keepdims=False)
    got_h = h_rows
    for d in range(1, n_col):
        chunk = lax.dynamic_index_in_dim(chunks, (col_index + d) % n_col, 0, keepdims=False)
        message = shifted(jnp.concatenate([chunk, h_rows]), "col", d)
        mine_w = mine_w + message[:share]
        got_h = got_h + message[share:]
    h_total = from_rows(got_h, rank)

    w_rows_sum = as_rows(w_sum, width)
    messages = [
        jnp.concatenate([x[:, p * half:(p + 1) * half] for x in numer_h_stack + [w_rows_sum]])
        for p in range(n_sub)
    ]
    def piece_message(k):
        want = (sub_index + k) % n_sub
        chosen = messages[0]
        for p in range(1, n_sub):
            chosen = jnp.where(want == p, messages[p], chosen)
        return chosen
    reduced = piece_message(0)
    for k in range(1, n_sub):
        reduced = reduced + shifted(piece_message(k), "sub", k)
    extra = reduced[n_row * rank:]
    mine_h = reduced[:rank]
    got_w = extra
    for d in reversed(range(1, n_row)):
        message = shifted(jnp.concatenate([reduced[d * rank:(d + 1) * rank], extra]), "row", d)
        mine_h = mine_h + message[:rank]
        got_w = got_w + message[rank:]
    final = jnp.concatenate([mine_h, got_w])
    total = assemble([final] + [shifted(final, "sub", k) for k in range(1, n_sub)], sub_index, n_sub, 1)
    numer_h = total[:rank]
    w_total = from_rows(total[rank:], rank)

    h_new = h_factor.astype(jnp.float32) * numer_h / w_total[:, None]
    w_part = lax.dynamic_slice_in_dim(w_tile, col_index * share, share, 0).astype(jnp.float32)
    w_new = (w_part * mine_w / h_total[None, :])[None]
    return (w_new, h_new)


def solution(mesh):
    placed = (
        P(("grp", "row", "sub"), "col", None, None, None, None),
        P(("grp", "row", "sub"), "col", None, None),
        P(("grp", "row", "sub"), "col", None),
        P(("grp", "row", "sub"), None, None),
        P(None, ("grp", "row", "col")),
    )
    return jax.shard_map(
        body,
        mesh=mesh,
        in_specs=placed,
        out_specs=(P(("grp", "row", "sub"), "col", None), P(None, ("grp", "row", "col"))),
        check_vma=False,
    )
```

```python
import jax
import jax.numpy as jnp
from jax import lax
from jax.sharding import PartitionSpec as P


def shifted(value, axis, by):
    length = lax.axis_size(axis)
    return lax.ppermute(value, axis, [(i, (i + by) % length) for i in range(length)])


def as_rows(vector, width):
    size = vector.shape[0]
    rows = -(-size // width)
    flat = jnp.pad(vector, (0, rows * width - size)).reshape(rows, width)
    return jnp.pad(flat, ((0, (-rows) % 8), (0, 0)))


def from_rows(rows, size):
    return rows.reshape(-1)[:size]


def assemble(pieces, index, count, axis):
    out = []
    for j in range(count):
        want = (index - j) % count
        chosen = pieces[0]
        for k in range(1, count):
            chosen = jnp.where(want == k, pieces[k], chosen)
        out.append(chosen)
    return jnp.concatenate(out, axis=axis)


def dense_terms(values, lists, counts, w_tile, h_stack, row_index):
    row_blocks, stored, width = values.shape[0], values.shape[1], values.shape[2]
    n_row, rank = h_stack.shape[0], h_stack.shape[1]
    tile_rows = w_tile.shape[0]
    h_rest = jnp.concatenate([h_stack[d] for d in range(1, n_row)], axis=1)
    product = jnp.concatenate(
        [
            jnp.dot(w_tile, h_stack[0], preferred_element_type=jnp.float32),
            jnp.dot(w_tile, h_rest, preferred_element_type=jnp.float32),
        ],
        axis=1,
    )
    chunks = []
    for d in range(n_row):
        block = (row_index - d) % n_row
        a_d = jnp.zeros((row_blocks, width, width), values.dtype)
        covered = jnp.zeros((row_blocks,), jnp.bool_)
        for slot in range(stored):
            match = (lists[:, slot] == block) & (slot < counts)
            a_d = jnp.where(match[:, None, None], values[:, slot], a_d)
            covered = covered | match
        p_d = product[:, d * width:(d + 1) * width].reshape(row_blocks, width, width)
        r_d = jnp.where(covered[:, None, None], a_d.astype(jnp.float32) / p_d, 0.0)
        chunks.append(r_d.astype(jnp.bfloat16).reshape(tile_rows, width))
    ratios_rest = jnp.concatenate(chunks[1:], axis=1)
    numer_h_all = jnp.concatenate(
        [
            jnp.einsum("ik,ij->kj", w_tile, chunks[0], preferred_element_type=jnp.float32),
            jnp.einsum("ik,ij->kj", w_tile, ratios_rest, preferred_element_type=jnp.float32),
        ],
        axis=1,
    )
    numer_w = jnp.einsum(
        "ij,kj->ik", chunks[0], h_stack[0], preferred_element_type=jnp.float32
    ) + jnp.einsum("ij,kj->ik", ratios_rest, h_rest, preferred_element_type=jnp.float32)
    starts = [((-e) % n_row) * width for e in range(n_row)]
    return [numer_h_all[:, s:s + width] for s in starts], numer_w


def slot_terms(values, lists, counts, w_tile, h_stack, row_index):
    row_blocks, stored, width = values.shape[0], values.shape[1], values.shape[2]
    n_row, rank = h_stack.shape[0], h_stack.shape[1]
    tile_rows = w_tile.shape[0]
    w_rows = w_tile.reshape(row_blocks, width, rank)
    numer_h_stack = jnp.zeros((n_row, rank, width), jnp.float32)
    parts_w = []
    for brow in range(row_blocks):
        part_w = jnp.zeros((width, rank), jnp.float32)
        for slot in range(stored):
            target = lists[brow, slot]
            live = slot < counts[brow]
            h_block = lax.dynamic_index_in_dim(
                h_stack, (row_index - target) % n_row, 0, keepdims=False
            )
            product = jnp.dot(w_rows[brow], h_block, preferred_element_type=jnp.float32)
            ratios = (values[brow, slot].astype(jnp.float32) / product).astype(jnp.bfloat16)
            ratios = jnp.where(live, ratios, jnp.zeros_like(ratios))
            part_h = jnp.einsum(
                "ik,ij->kj", w_rows[brow], ratios, preferred_element_type=jnp.float32
            )
            part_w = part_w + jnp.einsum(
                "ij,kj->ik", ratios, h_block, preferred_element_type=jnp.float32
            )
            offset = (target - row_index) % n_row
            old = lax.dynamic_index_in_dim(numer_h_stack, offset, 0, keepdims=True)
            numer_h_stack = lax.dynamic_update_index_in_dim(
                numer_h_stack, old + part_h[None], offset, 0
            )
        parts_w.append(part_w)
    numer_w = jnp.stack(parts_w).reshape(tile_rows, rank)
    return [numer_h_stack[e] for e in range(n_row)], numer_w


def body(a_blocks, block_list, block_count, w_factor, h_factor):
    values = a_blocks[0, 0]
    lists = block_list[0, 0]
    counts = block_count[0, 0]
    w_tile = w_factor[0]
    row_blocks, stored, width = values.shape[0], values.shape[1], values.shape[2]
    rank = w_tile.shape[1]
    tile_rows = w_tile.shape[0]
    n_row = lax.axis_size("row")
    n_col = lax.axis_size("col")
    n_sub = lax.axis_size("sub")
    row_index = lax.axis_index("row")
    col_index = lax.axis_index("col")

    sub_index = lax.axis_index("sub")
    half = width // n_sub
    own_piece = lax.dynamic_slice_in_dim(h_factor, sub_index * half, half, 1)
    arrived = {d: shifted(own_piece, "row", d) for d in reversed(range(1, n_row))}
    fetched = jnp.stack([arrived[d] for d in range(1, n_row)])
    swapped = [fetched] + [shifted(fetched, "sub", k) for k in range(1, n_sub)]
    others = assemble(swapped, sub_index, n_sub, 2)
    h_stack = jnp.concatenate([h_factor[None], others])
    h_sum = jnp.sum(h_stack.astype(jnp.float32), axis=(0, 2))
    w_sum = jnp.sum(w_tile.astype(jnp.float32), axis=0)

    if tile_rows * n_row * width * 4 <= (8 << 20):
        numer_h_stack, numer_w = dense_terms(values, lists, counts, w_tile, h_stack, row_index)
    else:
        numer_h_stack, numer_w = slot_terms(values, lists, counts, w_tile, h_stack, row_index)

    share = tile_rows // n_col
    chunks = numer_w.reshape(n_col, share, rank)
    h_rows = as_rows(h_sum, rank)
    mine_w = lax.dynamic_index_in_dim(chunks, col_index, 0, keepdims=False)
    got_h = h_rows
    for d in range(1, n_col):
        chunk = lax.dynamic_index_in_dim(chunks, (col_index + d) % n_col, 0, keepdims=False)
        message = shifted(jnp.concatenate([chunk, h_rows]), "col", d)
        mine_w = mine_w + message[:share]
        got_h = got_h + message[share:]
    h_total = from_rows(got_h, rank)

    w_rows_sum = as_rows(w_sum, width)
    messages = [
        jnp.concatenate([x[:, p * half:(p + 1) * half] for x in numer_h_stack + [w_rows_sum]])
        for p in range(n_sub)
    ]
    def piece_message(k):
        want = (sub_index + k) % n_sub
        chosen = messages[0]
        for p in range(1, n_sub):
            chosen = jnp.where(want == p, messages[p], chosen)
        return chosen
    reduced = piece_message(0)
    for k in range(1, n_sub):
        reduced = reduced + shifted(piece_message(k), "sub", k)
    extra = reduced[n_row * rank:]
    mine_h = reduced[:rank]
    got_w = extra
    for d in range(1, n_row):
        message = shifted(jnp.concatenate([reduced[d * rank:(d + 1) * rank], extra]), "row", d)
        mine_h = mine_h + message[:rank]
        got_w = got_w + message[rank:]
    final = jnp.concatenate([mine_h, got_w])
    total = assemble([final] + [shifted(final, "sub", k) for k in range(1, n_sub)], sub_index, n_sub, 1)
    numer_h = total[:rank]
    w_total = from_rows(total[rank:], rank)

    h_new = h_factor.astype(jnp.float32) * numer_h / w_total[:, None]
    w_part = lax.dynamic_slice_in_dim(w_tile, col_index * share, share, 0).astype(jnp.float32)
    w_new = (w_part * mine_w / h_total[None, :])[None]
    return (w_new, h_new)


def solution(mesh):
    placed = (
        P(("grp", "row", "sub"), "col", None, None, None, None),
        P(("grp", "row", "sub"), "col", None, None),
        P(("grp", "row", "sub"), "col", None),
        P(("grp", "row", "sub"), None, None),
        P(None, ("grp", "row", "col")),
    )
    return jax.shard_map(
        body,
        mesh=mesh,
        in_specs=placed,
        out_specs=(P(("grp", "row", "sub"), "col", None), P(None, ("grp", "row", "col"))),
        check_vma=False,
    )
```

```python
import jax
import jax.numpy as jnp
from jax import lax
from jax.sharding import PartitionSpec as P


def shifted(value, axis, by):
    length = lax.axis_size(axis)
    return lax.ppermute(value, axis, [(i, (i + by) % length) for i in range(length)])


def as_rows(vector, width):
    size = vector.shape[0]
    rows = -(-size // width)
    flat = jnp.pad(vector, (0, rows * width - size)).reshape(rows, width)
    return jnp.pad(flat, ((0, (-rows) % 8), (0, 0)))


def from_rows(rows, size):
    return rows.reshape(-1)[:size]


def assemble(pieces, index, count, axis):
    out = []
    for j in range(count):
        want = (index - j) % count
        chosen = pieces[0]
        for k in range(1, count):
            chosen = jnp.where(want == k, pieces[k], chosen)
        out.append(chosen)
    return jnp.concatenate(out, axis=axis)


def dense_terms(values, lists, counts, w_tile, h_stack, row_index):
    row_blocks, stored, width = values.shape[0], values.shape[1], values.shape[2]
    n_row, rank = h_stack.shape[0], h_stack.shape[1]
    tile_rows = w_tile.shape[0]
    h_rest = jnp.concatenate([h_stack[d] for d in range(1, n_row)], axis=1)
    product = jnp.concatenate(
        [
            jnp.dot(w_tile, h_stack[0], preferred_element_type=jnp.float32),
            jnp.dot(w_tile, h_rest, preferred_element_type=jnp.float32),
        ],
        axis=1,
    )
    chunks = []
    for d in range(n_row):
        block = (row_index - d) % n_row
        a_d = jnp.zeros((row_blocks, width, width), values.dtype)
        covered = jnp.zeros((row_blocks,), jnp.bool_)
        for slot in range(stored):
            match = (lists[:, slot] == block) & (slot < counts)
            a_d = jnp.where(match[:, None, None], values[:, slot], a_d)
            covered = covered | match
        p_d = product[:, d * width:(d + 1) * width].reshape(row_blocks, width, width)
        r_d = jnp.where(covered[:, None, None], a_d.astype(jnp.float32) / p_d, 0.0)
        chunks.append(r_d.astype(jnp.bfloat16).reshape(tile_rows, width))
    ratios_rest = jnp.concatenate(chunks[1:], axis=1)
    numer_h_all = jnp.concatenate(
        [
            jnp.einsum("ik,ij->kj", w_tile, chunks[0], preferred_element_type=jnp.float32),
            jnp.einsum("ik,ij->kj", w_tile, ratios_rest, preferred_element_type=jnp.float32),
        ],
        axis=1,
    )
    numer_w = jnp.einsum(
        "ij,kj->ik", chunks[0], h_stack[0], preferred_element_type=jnp.float32
    ) + jnp.einsum("ij,kj->ik", ratios_rest, h_rest, preferred_element_type=jnp.float32)
    starts = [((-e) % n_row) * width for e in range(n_row)]
    return [numer_h_all[:, s:s + width] for s in starts], numer_w


def slot_terms(values, lists, counts, w_tile, h_stack, row_index):
    row_blocks, stored, width = values.shape[0], values.shape[1], values.shape[2]
    n_row, rank = h_stack.shape[0], h_stack.shape[1]
    tile_rows = w_tile.shape[0]
    w_rows = w_tile.reshape(row_blocks, width, rank)
    numer_h_stack = jnp.zeros((n_row, rank, width), jnp.float32)
    parts_w = []
    for brow in range(row_blocks):
        part_w = jnp.zeros((width, rank), jnp.float32)
        for slot in range(stored):
            target = lists[brow, slot]
            live = slot < counts[brow]
            h_block = lax.dynamic_index_in_dim(
                h_stack, (row_index - target) % n_row, 0, keepdims=False
            )
            product = jnp.dot(w_rows[brow], h_block, preferred_element_type=jnp.float32)
            ratios = (values[brow, slot].astype(jnp.float32) / product).astype(jnp.bfloat16)
            ratios = jnp.where(live, ratios, jnp.zeros_like(ratios))
            part_h = jnp.einsum(
                "ik,ij->kj", w_rows[brow], ratios, preferred_element_type=jnp.float32
            )
            part_w = part_w + jnp.einsum(
                "ij,kj->ik", ratios, h_block, preferred_element_type=jnp.float32
            )
            offset = (target - row_index) % n_row
            old = lax.dynamic_index_in_dim(numer_h_stack, offset, 0, keepdims=True)
            numer_h_stack = lax.dynamic_update_index_in_dim(
                numer_h_stack, old + part_h[None], offset, 0
            )
        parts_w.append(part_w)
    numer_w = jnp.stack(parts_w).reshape(tile_rows, rank)
    return [numer_h_stack[e] for e in range(n_row)], numer_w


def body(a_blocks, block_list, block_count, w_factor, h_factor):
    values = a_blocks[0, 0]
    lists = block_list[0, 0]
    counts = block_count[0, 0]
    w_tile = w_factor[0]
    row_blocks, stored, width = values.shape[0], values.shape[1], values.shape[2]
    rank = w_tile.shape[1]
    tile_rows = w_tile.shape[0]
    n_row = lax.axis_size("row")
    n_col = lax.axis_size("col")
    n_sub = lax.axis_size("sub")
    row_index = lax.axis_index("row")
    col_index = lax.axis_index("col")

    sub_index = lax.axis_index("sub")
    half = width // n_sub
    own_piece = h_factor[:, :half]
    for p in range(1, n_sub):
        own_piece = jnp.where(sub_index == p, h_factor[:, p * half:(p + 1) * half], own_piece)
    arrived = {d: shifted(own_piece, "row", d) for d in reversed(range(1, n_row))}
    fetched = jnp.stack([arrived[d] for d in range(1, n_row)])
    swapped = [fetched] + [shifted(fetched, "sub", k) for k in range(1, n_sub)]
    others = assemble(swapped, sub_index, n_sub, 2)
    h_stack = jnp.concatenate([h_factor[None], others])
    h_sum = jnp.sum(h_stack.astype(jnp.float32), axis=(0, 2))
    w_sum = jnp.sum(w_tile.astype(jnp.float32), axis=0)

    if tile_rows * n_row * width * 4 <= (8 << 20):
        numer_h_stack, numer_w = dense_terms(values, lists, counts, w_tile, h_stack, row_index)
    else:
        numer_h_stack, numer_w = slot_terms(values, lists, counts, w_tile, h_stack, row_index)

    share = tile_rows // n_col
    chunks = numer_w.reshape(n_col, share, rank)
    h_rows = as_rows(h_sum, rank)
    mine_w = lax.dynamic_index_in_dim(chunks, col_index, 0, keepdims=False)
    got_h = h_rows
    for d in range(1, n_col):
        chunk = lax.dynamic_index_in_dim(chunks, (col_index + d) % n_col, 0, keepdims=False)
        message = shifted(jnp.concatenate([chunk, h_rows]), "col", d)
        mine_w = mine_w + message[:share]
        got_h = got_h + message[share:]
    h_total = from_rows(got_h, rank)

    w_rows_sum = as_rows(w_sum, width)
    messages = [
        jnp.concatenate([x[:, p * half:(p + 1) * half] for x in numer_h_stack + [w_rows_sum]])
        for p in range(n_sub)
    ]
    def piece_message(k):
        want = (sub_index + k) % n_sub
        chosen = messages[0]
        for p in range(1, n_sub):
            chosen = jnp.where(want == p, messages[p], chosen)
        return chosen
    reduced = piece_message(0)
    for k in range(1, n_sub):
        reduced = reduced + shifted(piece_message(k), "sub", k)
    extra = reduced[n_row * rank:]
    mine_h = reduced[:rank]
    got_w = extra
    for d in reversed(range(1, n_row)):
        message = shifted(jnp.concatenate([reduced[d * rank:(d + 1) * rank], extra]), "row", d)
        mine_h = mine_h + message[:rank]
        got_w = got_w + message[rank:]
    final = jnp.concatenate([mine_h, got_w])
    total = assemble([final] + [shifted(final, "sub", k) for k in range(1, n_sub)], sub_index, n_sub, 1)
    numer_h = total[:rank]
    w_total = from_rows(total[rank:], rank)

    h_new = h_factor.astype(jnp.float32) * numer_h / w_total[:, None]
    w_part = lax.dynamic_slice_in_dim(w_tile, col_index * share, share, 0).astype(jnp.float32)
    w_new = (w_part * mine_w / h_total[None, :])[None]
    return (w_new, h_new)


def solution(mesh):
    placed = (
        P(("grp", "row", "sub"), "col", None, None, None, None),
        P(("grp", "row", "sub"), "col", None, None),
        P(("grp", "row", "sub"), "col", None),
        P(("grp", "row", "sub"), None, None),
        P(None, ("grp", "row", "col")),
    )
    return jax.shard_map(
        body,
        mesh=mesh,
        in_specs=placed,
        out_specs=(P(("grp", "row", "sub"), "col", None), P(None, ("grp", "row", "col"))),
        check_vma=False,
    )
```

```python
import jax
import jax.numpy as jnp
from jax import lax
from jax.sharding import PartitionSpec as P


def shifted(value, axis, by):
    length = lax.axis_size(axis)
    return lax.ppermute(value, axis, [(i, (i + by) % length) for i in range(length)])


def as_rows(vector, width):
    size = vector.shape[0]
    rows = -(-size // width)
    flat = jnp.pad(vector, (0, rows * width - size)).reshape(rows, width)
    return jnp.pad(flat, ((0, (-rows) % 8), (0, 0)))


def from_rows(rows, size):
    return rows.reshape(-1)[:size]


def assemble(pieces, index, count, axis):
    out = []
    for j in range(count):
        want = (index - j) % count
        chosen = pieces[0]
        for k in range(1, count):
            chosen = jnp.where(want == k, pieces[k], chosen)
        out.append(chosen)
    return jnp.concatenate(out, axis=axis)


def dense_terms(values, lists, counts, w_tile, h_stack, row_index):
    row_blocks, stored, width = values.shape[0], values.shape[1], values.shape[2]
    n_row, rank = h_stack.shape[0], h_stack.shape[1]
    tile_rows = w_tile.shape[0]
    h_rest = jnp.concatenate([h_stack[d] for d in range(1, n_row)], axis=1)
    product = jnp.concatenate(
        [
            jnp.dot(w_tile, h_stack[0], preferred_element_type=jnp.float32),
            jnp.dot(w_tile, h_rest, preferred_element_type=jnp.float32),
        ],
        axis=1,
    )
    chunks = []
    for d in range(n_row):
        block = (row_index - d) % n_row
        a_d = jnp.zeros((row_blocks, width, width), values.dtype)
        covered = jnp.zeros((row_blocks,), jnp.bool_)
        for slot in range(stored):
            match = (lists[:, slot] == block) & (slot < counts)
            a_d = jnp.where(match[:, None, None], values[:, slot], a_d)
            covered = covered | match
        p_d = product[:, d * width:(d + 1) * width].reshape(row_blocks, width, width)
        r_d = jnp.where(covered[:, None, None], a_d.astype(jnp.float32) / p_d, 0.0)
        chunks.append(r_d.astype(jnp.bfloat16).reshape(tile_rows, width))
    ratios_rest = jnp.concatenate(chunks[1:], axis=1)
    numer_h_all = jnp.concatenate(
        [
            jnp.einsum("ik,ij->kj", w_tile, chunks[0], preferred_element_type=jnp.float32),
            jnp.einsum("ik,ij->kj", w_tile, ratios_rest, preferred_element_type=jnp.float32),
        ],
        axis=1,
    )
    numer_w = (chunks[0], h_stack[0], ratios_rest, h_rest)
    starts = [((-e) % n_row) * width for e in range(n_row)]
    return [numer_h_all[:, s:s + width] for s in starts], numer_w


def slot_terms(values, lists, counts, w_tile, h_stack, row_index):
    row_blocks, stored, width = values.shape[0], values.shape[1], values.shape[2]
    n_row, rank = h_stack.shape[0], h_stack.shape[1]
    tile_rows = w_tile.shape[0]
    w_rows = w_tile.reshape(row_blocks, width, rank)
    numer_h_stack = jnp.zeros((n_row, rank, width), jnp.float32)
    parts_w = []
    for brow in range(row_blocks):
        part_w = jnp.zeros((width, rank), jnp.float32)
        for slot in range(stored):
            target = lists[brow, slot]
            live = slot < counts[brow]
            h_block = lax.dynamic_index_in_dim(
                h_stack, (row_index - target) % n_row, 0, keepdims=False
            )
            product = jnp.dot(w_rows[brow], h_block, preferred_element_type=jnp.float32)
            ratios = (values[brow, slot].astype(jnp.float32) / product).astype(jnp.bfloat16)
            ratios = jnp.where(live, ratios, jnp.zeros_like(ratios))
            part_h = jnp.einsum(
                "ik,ij->kj", w_rows[brow], ratios, preferred_element_type=jnp.float32
            )
            part_w = part_w + jnp.einsum(
                "ij,kj->ik", ratios, h_block, preferred_element_type=jnp.float32
            )
            offset = (target - row_index) % n_row
            old = lax.dynamic_index_in_dim(numer_h_stack, offset, 0, keepdims=True)
            numer_h_stack = lax.dynamic_update_index_in_dim(
                numer_h_stack, old + part_h[None], offset, 0
            )
        parts_w.append(part_w)
    numer_w = jnp.stack(parts_w).reshape(tile_rows, rank)
    return [numer_h_stack[e] for e in range(n_row)], numer_w


def body(a_blocks, block_list, block_count, w_factor, h_factor):
    values = a_blocks[0, 0]
    lists = block_list[0, 0]
    counts = block_count[0, 0]
    w_tile = w_factor[0]
    row_blocks, stored, width = values.shape[0], values.shape[1], values.shape[2]
    rank = w_tile.shape[1]
    tile_rows = w_tile.shape[0]
    n_row = lax.axis_size("row")
    n_col = lax.axis_size("col")
    n_sub = lax.axis_size("sub")
    row_index = lax.axis_index("row")
    col_index = lax.axis_index("col")

    sub_index = lax.axis_index("sub")
    half = width // n_sub
    own_piece = h_factor[:, :half]
    for p in range(1, n_sub):
        own_piece = jnp.where(sub_index == p, h_factor[:, p * half:(p + 1) * half], own_piece)
    arrived = {d: shifted(own_piece, "row", d) for d in reversed(range(1, n_row))}
    fetched = jnp.stack([arrived[d] for d in range(1, n_row)])
    swapped = [fetched] + [shifted(fetched, "sub", k) for k in range(1, n_sub)]
    others = assemble(swapped, sub_index, n_sub, 2)
    h_stack = jnp.concatenate([h_factor[None], others])
    h_sum = jnp.sum(h_stack.astype(jnp.float32), axis=(0, 2))
    w_sum = jnp.sum(w_tile.astype(jnp.float32), axis=0)

    dense = tile_rows * n_row * width * 4 <= (8 << 20)
    if dense:
        numer_h_stack, w_inputs = dense_terms(values, lists, counts, w_tile, h_stack, row_index)
    else:
        numer_h_stack, numer_w = slot_terms(values, lists, counts, w_tile, h_stack, row_index)

    w_rows_sum = as_rows(w_sum, width)
    messages = [
        jnp.concatenate([x[:, p * half:(p + 1) * half] for x in numer_h_stack + [w_rows_sum]])
        for p in range(n_sub)
    ]
    if dense:
        messages, w_inputs = lax.optimization_barrier((messages, w_inputs))
        own_r, own_h, rest_r, rest_h = w_inputs
        numer_w = jnp.einsum(
            "ij,kj->ik", own_r, own_h, preferred_element_type=jnp.float32
        ) + jnp.einsum("ij,kj->ik", rest_r, rest_h, preferred_element_type=jnp.float32)

    share = tile_rows // n_col
    chunks = numer_w.reshape(n_col, share, rank)
    h_rows = as_rows(h_sum, rank)
    mine_w = lax.dynamic_index_in_dim(chunks, col_index, 0, keepdims=False)
    got_h = h_rows
    for d in range(1, n_col):
        chunk = lax.dynamic_index_in_dim(chunks, (col_index + d) % n_col, 0, keepdims=False)
        message = shifted(jnp.concatenate([chunk, h_rows]), "col", d)
        mine_w = mine_w + message[:share]
        got_h = got_h + message[share:]
    h_total = from_rows(got_h, rank)

    def piece_message(k):
        want = (sub_index + k) % n_sub
        chosen = messages[0]
        for p in range(1, n_sub):
            chosen = jnp.where(want == p, messages[p], chosen)
        return chosen
    reduced = piece_message(0)
    for k in range(1, n_sub):
        reduced = reduced + shifted(piece_message(k), "sub", k)
    extra = reduced[n_row * rank:]
    mine_h = reduced[:rank]
    got_w = extra
    for d in reversed(range(1, n_row)):
        message = shifted(jnp.concatenate([reduced[d * rank:(d + 1) * rank], extra]), "row", d)
        mine_h = mine_h + message[:rank]
        got_w = got_w + message[rank:]
    final = jnp.concatenate([mine_h, got_w])
    total = assemble([final] + [shifted(final, "sub", k) for k in range(1, n_sub)], sub_index, n_sub, 1)
    numer_h = total[:rank]
    w_total = from_rows(total[rank:], rank)

    h_new = h_factor.astype(jnp.float32) * numer_h / w_total[:, None]
    w_part = lax.dynamic_slice_in_dim(w_tile, col_index * share, share, 0).astype(jnp.float32)
    w_new = (w_part * mine_w / h_total[None, :])[None]
    return (w_new, h_new)


def solution(mesh):
    placed = (
        P(("grp", "row", "sub"), "col", None, None, None, None),
        P(("grp", "row", "sub"), "col", None, None),
        P(("grp", "row", "sub"), "col", None),
        P(("grp", "row", "sub"), None, None),
        P(None, ("grp", "row", "col")),
    )
    return jax.shard_map(
        body,
        mesh=mesh,
        in_specs=placed,
        out_specs=(P(("grp", "row", "sub"), "col", None), P(None, ("grp", "row", "col"))),
        check_vma=False,
    )
```

```python
import jax
import jax.numpy as jnp
from jax import lax
from jax.sharding import PartitionSpec as P


def shifted(value, axis, by):
    length = lax.axis_size(axis)
    return lax.ppermute(value, axis, [(i, (i + by) % length) for i in range(length)])


def as_rows(vector, width):
    size = vector.shape[0]
    rows = -(-size // width)
    flat = jnp.pad(vector, (0, rows * width - size)).reshape(rows, width)
    return jnp.pad(flat, ((0, (-rows) % 8), (0, 0)))


def from_rows(rows, size):
    return rows.reshape(-1)[:size]


def assemble(pieces, index, count, axis):
    out = []
    for j in range(count):
        want = (index - j) % count
        chosen = pieces[0]
        for k in range(1, count):
            chosen = jnp.where(want == k, pieces[k], chosen)
        out.append(chosen)
    return jnp.concatenate(out, axis=axis)


def dense_terms(values, lists, counts, w_tile, h_stack, row_index):
    row_blocks, stored, width = values.shape[0], values.shape[1], values.shape[2]
    n_row, rank = h_stack.shape[0], h_stack.shape[1]
    tile_rows = w_tile.shape[0]
    h_rest = jnp.concatenate([h_stack[d] for d in range(1, n_row)], axis=1)
    product = jnp.concatenate(
        [
            jnp.dot(w_tile, h_stack[0], preferred_element_type=jnp.float32),
            jnp.dot(w_tile, h_rest, preferred_element_type=jnp.float32),
        ],
        axis=1,
    )
    chunks = []
    for d in range(n_row):
        block = (row_index - d) % n_row
        a_d = jnp.zeros((row_blocks, width, width), values.dtype)
        covered = jnp.zeros((row_blocks,), jnp.bool_)
        for slot in range(stored):
            match = (lists[:, slot] == block) & (slot < counts)
            a_d = jnp.where(match[:, None, None], values[:, slot], a_d)
            covered = covered | match
        p_d = product[:, d * width:(d + 1) * width].reshape(row_blocks, width, width)
        r_d = jnp.where(covered[:, None, None], a_d.astype(jnp.float32) / p_d, 0.0)
        chunks.append(r_d.astype(jnp.bfloat16).reshape(tile_rows, width))
    ratios_rest = jnp.concatenate(chunks[1:], axis=1)
    numer_h_all = jnp.concatenate(
        [
            jnp.einsum("ik,ij->kj", w_tile, chunks[0], preferred_element_type=jnp.float32),
            jnp.einsum("ik,ij->kj", w_tile, ratios_rest, preferred_element_type=jnp.float32),
        ],
        axis=1,
    )
    numer_w = jnp.einsum(
        "ij,kj->ik", chunks[0], h_stack[0], preferred_element_type=jnp.float32
    ) + jnp.einsum("ij,kj->ik", ratios_rest, h_rest, preferred_element_type=jnp.float32)
    starts = [((-e) % n_row) * width for e in range(n_row)]
    return [numer_h_all[:, s:s + width] for s in starts], numer_w


def slot_terms(values, lists, counts, w_tile, h_stack, row_index):
    row_blocks, stored, width = values.shape[0], values.shape[1], values.shape[2]
    n_row, rank = h_stack.shape[0], h_stack.shape[1]
    tile_rows = w_tile.shape[0]
    w_rows = w_tile.reshape(row_blocks, width, rank)
    numer_h_stack = jnp.zeros((n_row, rank, width), jnp.float32)
    parts_w = []
    for brow in range(row_blocks):
        part_w = jnp.zeros((width, rank), jnp.float32)
        for slot in range(stored):
            target = lists[brow, slot]
            live = slot < counts[brow]
            h_block = lax.dynamic_index_in_dim(
                h_stack, (row_index - target) % n_row, 0, keepdims=False
            )
            product = jnp.dot(w_rows[brow], h_block, preferred_element_type=jnp.float32)
            ratios = (values[brow, slot].astype(jnp.float32) / product).astype(jnp.bfloat16)
            ratios = jnp.where(live, ratios, jnp.zeros_like(ratios))
            part_h = jnp.einsum(
                "ik,ij->kj", w_rows[brow], ratios, preferred_element_type=jnp.float32
            )
            part_w = part_w + jnp.einsum(
                "ij,kj->ik", ratios, h_block, preferred_element_type=jnp.float32
            )
            offset = (target - row_index) % n_row
            old = lax.dynamic_index_in_dim(numer_h_stack, offset, 0, keepdims=True)
            numer_h_stack = lax.dynamic_update_index_in_dim(
                numer_h_stack, old + part_h[None], offset, 0
            )
        parts_w.append(part_w)
    numer_w = jnp.stack(parts_w).reshape(tile_rows, rank)
    return [numer_h_stack[e] for e in range(n_row)], numer_w


def split_terms(values, lists, counts, w_tile, h_own, fetched, swapped, row_index, sub_index):
    row_blocks, stored, width = values.shape[0], values.shape[1], values.shape[2]
    n_row, rank = fetched.shape[0] + 1, h_own.shape[0]
    tile_rows = w_tile.shape[0]
    half = fetched.shape[2]

    def placed(d):
        block = (row_index - d) % n_row
        a_d = jnp.zeros((row_blocks, width, width), values.dtype)
        covered = jnp.zeros((row_blocks,), jnp.bool_)
        for slot in range(stored):
            match = (lists[:, slot] == block) & (slot < counts)
            a_d = jnp.where(match[:, None, None], values[:, slot], a_d)
            covered = covered | match
        return a_d, covered

    def ratios_of(a_d, covered, p_d, cols):
        p_d = p_d.reshape(row_blocks, width, cols)
        r_d = jnp.where(covered[:, None, None], a_d.astype(jnp.float32) / p_d, 0.0)
        return r_d.astype(jnp.bfloat16).reshape(tile_rows, cols)

    def piece_of(a_d, first):
        lo, hi = a_d[:, :, :half], a_d[:, :, half:]
        return jnp.where(sub_index == 0, lo, hi) if first else jnp.where(sub_index == 0, hi, lo)

    a_own, c_own = placed(0)
    r_own = ratios_of(a_own, c_own, jnp.dot(w_tile, h_own, preferred_element_type=jnp.float32), width)
    nh_own = jnp.einsum("ik,ij->kj", w_tile, r_own, preferred_element_type=jnp.float32)
    nw = jnp.einsum("ij,kj->ik", r_own, h_own, preferred_element_type=jnp.float32)

    remote = [placed(d) for d in range(1, n_row)]
    halves = []
    for first, h_half in ((True, fetched), (False, swapped)):
        h_cols = jnp.concatenate([h_half[d] for d in range(n_row - 1)], axis=1)
        product = jnp.dot(w_tile, h_cols, preferred_element_type=jnp.float32)
        cols = [
            ratios_of(piece_of(a_d, first), cov, product[:, i * half:(i + 1) * half], half)
            for i, (a_d, cov) in enumerate(remote)
        ]
        ratios = jnp.concatenate(cols, axis=1)
        halves.append(jnp.einsum("ik,ij->kj", w_tile, ratios, preferred_element_type=jnp.float32))
        nw = nw + jnp.einsum("ij,kj->ik", ratios, h_cols, preferred_element_type=jnp.float32)
    chunks_h = [nh_own]
    for i in range(n_row - 1):
        a_part = halves[0][:, i * half:(i + 1) * half]
        b_part = halves[1][:, i * half:(i + 1) * half]
        chunks_h.append(assemble([a_part, b_part], sub_index, 2, 1))
    return [chunks_h[(-e) % n_row] for e in range(n_row)], nw


def body(a_blocks, block_list, block_count, w_factor, h_factor):
    values = a_blocks[0, 0]
    lists = block_list[0, 0]
    counts = block_count[0, 0]
    w_tile = w_factor[0]
    row_blocks, stored, width = values.shape[0], values.shape[1], values.shape[2]
    rank = w_tile.shape[1]
    tile_rows = w_tile.shape[0]
    n_row = lax.axis_size("row")
    n_col = lax.axis_size("col")
    n_sub = lax.axis_size("sub")
    row_index = lax.axis_index("row")
    col_index = lax.axis_index("col")

    sub_index = lax.axis_index("sub")
    half = width // n_sub
    own_piece = h_factor[:, :half]
    for p in range(1, n_sub):
        own_piece = jnp.where(sub_index == p, h_factor[:, p * half:(p + 1) * half], own_piece)
    arrived = {d: shifted(own_piece, "row", d) for d in reversed(range(1, n_row))}
    fetched = jnp.stack([arrived[d] for d in range(1, n_row)])
    swapped = [fetched] + [shifted(fetched, "sub", k) for k in range(1, n_sub)]
    others = assemble(swapped, sub_index, n_sub, 2)
    h_stack = jnp.concatenate([h_factor[None], others])
    h_sum = jnp.sum(h_stack.astype(jnp.float32), axis=(0, 2))
    w_sum = jnp.sum(w_tile.astype(jnp.float32), axis=0)

    if tile_rows * n_row * width * 4 <= (8 << 20) and n_sub == 2:
        numer_h_stack, numer_w = split_terms(
            values, lists, counts, w_tile, h_factor, fetched, swapped[1], row_index, sub_index
        )
    elif tile_rows * n_row * width * 4 <= (8 << 20):
        numer_h_stack, numer_w = dense_terms(values, lists, counts, w_tile, h_stack, row_index)
    else:
        numer_h_stack, numer_w = slot_terms(values, lists, counts, w_tile, h_stack, row_index)

    share = tile_rows // n_col
    chunks = numer_w.reshape(n_col, share, rank)
    h_rows = as_rows(h_sum, rank)
    mine_w = lax.dynamic_index_in_dim(chunks, col_index, 0, keepdims=False)
    got_h = h_rows
    for d in range(1, n_col):
        chunk = lax.dynamic_index_in_dim(chunks, (col_index + d) % n_col, 0, keepdims=False)
        message = shifted(jnp.concatenate([chunk, h_rows]), "col", d)
        mine_w = mine_w + message[:share]
        got_h = got_h + message[share:]
    h_total = from_rows(got_h, rank)

    w_rows_sum = as_rows(w_sum, width)
    messages = [
        jnp.concatenate([x[:, p * half:(p + 1) * half] for x in numer_h_stack + [w_rows_sum]])
        for p in range(n_sub)
    ]
    def piece_message(k):
        want = (sub_index + k) % n_sub
        chosen = messages[0]
        for p in range(1, n_sub):
            chosen = jnp.where(want == p, messages[p], chosen)
        return chosen
    reduced = piece_message(0)
    for k in range(1, n_sub):
        reduced = reduced + shifted(piece_message(k), "sub", k)
    extra = reduced[n_row * rank:]
    mine_h = reduced[:rank]
    got_w = extra
    for d in reversed(range(1, n_row)):
        message = shifted(jnp.concatenate([reduced[d * rank:(d + 1) * rank], extra]), "row", d)
        mine_h = mine_h + message[:rank]
        got_w = got_w + message[rank:]
    final = jnp.concatenate([mine_h, got_w])
    total = assemble([final] + [shifted(final, "sub", k) for k in range(1, n_sub)], sub_index, n_sub, 1)
    numer_h = total[:rank]
    w_total = from_rows(total[rank:], rank)

    h_new = h_factor.astype(jnp.float32) * numer_h / w_total[:, None]
    w_part = lax.dynamic_slice_in_dim(w_tile, col_index * share, share, 0).astype(jnp.float32)
    w_new = (w_part * mine_w / h_total[None, :])[None]
    return (w_new, h_new)


def solution(mesh):
    placed = (
        P(("grp", "row", "sub"), "col", None, None, None, None),
        P(("grp", "row", "sub"), "col", None, None),
        P(("grp", "row", "sub"), "col", None),
        P(("grp", "row", "sub"), None, None),
        P(None, ("grp", "row", "col")),
    )
    return jax.shard_map(
        body,
        mesh=mesh,
        in_specs=placed,
        out_specs=(P(("grp", "row", "sub"), "col", None), P(None, ("grp", "row", "col"))),
        check_vma=False,
    )
```

```python
import jax
import jax.numpy as jnp
from jax import lax
from jax.sharding import PartitionSpec as P


def shifted(value, axis, by):
    length = lax.axis_size(axis)
    return lax.ppermute(value, axis, [(i, (i + by) % length) for i in range(length)])


def as_rows(vector, width):
    size = vector.shape[0]
    rows = -(-size // width)
    flat = jnp.pad(vector, (0, rows * width - size)).reshape(rows, width)
    return jnp.pad(flat, ((0, (-rows) % 8), (0, 0)))


def from_rows(rows, size):
    return rows.reshape(-1)[:size]


def assemble(pieces, index, count, axis):
    out = []
    for j in range(count):
        want = (index - j) % count
        chosen = pieces[0]
        for k in range(1, count):
            chosen = jnp.where(want == k, pieces[k], chosen)
        out.append(chosen)
    return jnp.concatenate(out, axis=axis)


def dense_terms(values, lists, counts, w_tile, h_stack, row_index):
    row_blocks, stored, width = values.shape[0], values.shape[1], values.shape[2]
    n_row, rank = h_stack.shape[0], h_stack.shape[1]
    tile_rows = w_tile.shape[0]
    h_rest = jnp.concatenate([h_stack[d] for d in range(1, n_row)], axis=1)
    product = jnp.concatenate(
        [
            jnp.dot(w_tile, h_stack[0], preferred_element_type=jnp.float32),
            jnp.dot(w_tile, h_rest, preferred_element_type=jnp.float32),
        ],
        axis=1,
    )
    chunks = []
    for d in range(n_row):
        block = (row_index - d) % n_row
        a_d = jnp.zeros((row_blocks, width, width), values.dtype)
        covered = jnp.zeros((row_blocks,), jnp.bool_)
        for slot in range(stored):
            match = (lists[:, slot] == block) & (slot < counts)
            a_d = jnp.where(match[:, None, None], values[:, slot], a_d)
            covered = covered | match
        p_d = product[:, d * width:(d + 1) * width].reshape(row_blocks, width, width)
        r_d = jnp.where(covered[:, None, None], a_d.astype(jnp.float32) / p_d, 0.0)
        chunks.append(r_d.astype(jnp.bfloat16).reshape(tile_rows, width))
    ratios_rest = jnp.concatenate(chunks[1:], axis=1)
    numer_h_all = jnp.concatenate(
        [
            jnp.einsum("ik,ij->kj", w_tile, chunks[0], preferred_element_type=jnp.float32),
            jnp.einsum("ik,ij->kj", w_tile, ratios_rest, preferred_element_type=jnp.float32),
        ],
        axis=1,
    )
    numer_w = jnp.einsum(
        "ij,kj->ik", chunks[0], h_stack[0], preferred_element_type=jnp.float32
    ) + jnp.einsum("ij,kj->ik", ratios_rest, h_rest, preferred_element_type=jnp.float32)
    starts = [((-e) % n_row) * width for e in range(n_row)]
    return [numer_h_all[:, s:s + width] for s in starts], numer_w


def slot_terms(values, lists, counts, w_tile, h_stack, row_index):
    row_blocks, stored, width = values.shape[0], values.shape[1], values.shape[2]
    n_row, rank = h_stack.shape[0], h_stack.shape[1]
    tile_rows = w_tile.shape[0]
    w_rows = w_tile.reshape(row_blocks, width, rank)
    numer_h_stack = jnp.zeros((n_row, rank, width), jnp.float32)
    parts_w = []
    for brow in range(row_blocks):
        part_w = jnp.zeros((width, rank), jnp.float32)
        for slot in range(stored):
            target = lists[brow, slot]
            live = slot < counts[brow]
            h_block = lax.dynamic_index_in_dim(
                h_stack, (row_index - target) % n_row, 0, keepdims=False
            )
            product = jnp.dot(w_rows[brow], h_block, preferred_element_type=jnp.float32)
            ratios = (values[brow, slot].astype(jnp.float32) / product).astype(jnp.bfloat16)
            ratios = jnp.where(live, ratios, jnp.zeros_like(ratios))
            part_h = jnp.einsum(
                "ik,ij->kj", w_rows[brow], ratios, preferred_element_type=jnp.float32
            )
            part_w = part_w + jnp.einsum(
                "ij,kj->ik", ratios, h_block, preferred_element_type=jnp.float32
            )
            offset = (target - row_index) % n_row
            old = lax.dynamic_index_in_dim(numer_h_stack, offset, 0, keepdims=True)
            numer_h_stack = lax.dynamic_update_index_in_dim(
                numer_h_stack, old + part_h[None], offset, 0
            )
        parts_w.append(part_w)
    numer_w = jnp.stack(parts_w).reshape(tile_rows, rank)
    return [numer_h_stack[e] for e in range(n_row)], numer_w


def body(a_blocks, block_list, block_count, w_factor, h_factor):
    values = a_blocks[0, 0]
    lists = block_list[0, 0]
    counts = block_count[0, 0]
    w_tile = w_factor[0]
    row_blocks, stored, width = values.shape[0], values.shape[1], values.shape[2]
    rank = w_tile.shape[1]
    tile_rows = w_tile.shape[0]
    n_row = lax.axis_size("row")
    n_col = lax.axis_size("col")
    n_sub = lax.axis_size("sub")
    row_index = lax.axis_index("row")
    col_index = lax.axis_index("col")

    sub_index = lax.axis_index("sub")
    half = width // n_sub
    own_piece = h_factor[:, :half]
    for p in range(1, n_sub):
        own_piece = jnp.where(sub_index == p, h_factor[:, p * half:(p + 1) * half], own_piece)
    arrived = {d: shifted(own_piece, "row", d) for d in reversed(range(1, n_row))}
    fetched = jnp.stack([arrived[d] for d in range(1, n_row)])
    swapped = [fetched] + [shifted(fetched, "sub", k) for k in range(1, n_sub)]
    others = assemble(swapped, sub_index, n_sub, 2)
    h_stack = jnp.concatenate([h_factor[None], others])
    h_sum = jnp.sum(h_stack.astype(jnp.float32), axis=(0, 2))
    w_sum = jnp.sum(w_tile.astype(jnp.float32), axis=0)

    if tile_rows * n_row * width * 4 <= (8 << 20):
        numer_h_stack, numer_w = dense_terms(values, lists, counts, w_tile, h_stack, row_index)
    else:
        numer_h_stack, numer_w = slot_terms(values, lists, counts, w_tile, h_stack, row_index)

    share = tile_rows // n_col
    chunks = numer_w.reshape(n_col, share, rank)
    h_rows = as_rows(h_sum, rank)
    mine_w = lax.dynamic_index_in_dim(chunks, col_index, 0, keepdims=False)
    got_h = h_rows
    for d in range(1, n_col):
        chunk = lax.dynamic_index_in_dim(chunks, (col_index + d) % n_col, 0, keepdims=False)
        message = shifted(jnp.concatenate([chunk, h_rows]), "col", d)
        mine_w = mine_w + message[:share]
        got_h = got_h + message[share:]
    h_total = from_rows(got_h, rank)

    w_rows_sum = as_rows(w_sum, half)
    messages = [
        jnp.concatenate([x[:, p * half:(p + 1) * half] for x in numer_h_stack] + [w_rows_sum])
        for p in range(n_sub)
    ]
    def piece_message(k):
        want = (sub_index + k) % n_sub
        chosen = messages[0]
        for p in range(1, n_sub):
            chosen = jnp.where(want == p, messages[p], chosen)
        return chosen
    reduced = piece_message(0)
    for k in range(1, n_sub):
        reduced = reduced + shifted(piece_message(k), "sub", k)
    extra = reduced[n_row * rank:]
    mine_h = reduced[:rank]
    got_w = extra
    for d in reversed(range(1, n_row)):
        message = shifted(jnp.concatenate([reduced[d * rank:(d + 1) * rank], extra]), "row", d)
        mine_h = mine_h + message[:rank]
        got_w = got_w + message[rank:]
    w_total = from_rows(got_w, rank)
    h_piece = own_piece.astype(jnp.float32) * mine_h / w_total[:, None]
    h_new = assemble(
        [h_piece] + [shifted(h_piece, "sub", k) for k in range(1, n_sub)], sub_index, n_sub, 1
    )
    w_part = lax.dynamic_slice_in_dim(w_tile, col_index * share, share, 0).astype(jnp.float32)
    w_new = (w_part * mine_w / h_total[None, :])[None]
    return (w_new, h_new)


def solution(mesh):
    placed = (
        P(("grp", "row", "sub"), "col", None, None, None, None),
        P(("grp", "row", "sub"), "col", None, None),
        P(("grp", "row", "sub"), "col", None),
        P(("grp", "row", "sub"), None, None),
        P(None, ("grp", "row", "col")),
    )
    return jax.shard_map(
        body,
        mesh=mesh,
        in_specs=placed,
        out_specs=(P(("grp", "row", "sub"), "col", None), P(None, ("grp", "row", "col"))),
        check_vma=False,
    )
```

```python
import jax
import jax.numpy as jnp
from jax import lax
from jax.sharding import PartitionSpec as P


def shifted(value, axis, by):
    length = lax.axis_size(axis)
    return lax.ppermute(value, axis, [(i, (i + by) % length) for i in range(length)])


def as_rows(vector, width):
    size = vector.shape[0]
    rows = -(-size // width)
    flat = jnp.pad(vector, (0, rows * width - size)).reshape(rows, width)
    return jnp.pad(flat, ((0, (-rows) % 8), (0, 0)))


def from_rows(rows, size):
    return rows.reshape(-1)[:size]


def assemble(pieces, index, count, axis):
    out = []
    for j in range(count):
        want = (index - j) % count
        chosen = pieces[0]
        for k in range(1, count):
            chosen = jnp.where(want == k, pieces[k], chosen)
        out.append(chosen)
    return jnp.concatenate(out, axis=axis)


def dense_terms(values, lists, counts, w_tile, h_stack, row_index):
    row_blocks, stored, width = values.shape[0], values.shape[1], values.shape[2]
    n_row, rank = h_stack.shape[0], h_stack.shape[1]
    tile_rows = w_tile.shape[0]
    h_rest = jnp.concatenate([h_stack[d] for d in range(1, n_row)], axis=1)
    product = jnp.concatenate(
        [
            jnp.dot(w_tile, h_stack[0], preferred_element_type=jnp.float32),
            jnp.dot(w_tile, h_rest, preferred_element_type=jnp.float32),
        ],
        axis=1,
    )
    chunks = []
    for d in range(n_row):
        block = (row_index - d) % n_row
        a_d = jnp.zeros((row_blocks, width, width), values.dtype)
        covered = jnp.zeros((row_blocks,), jnp.bool_)
        for slot in range(stored):
            match = (lists[:, slot] == block) & (slot < counts)
            a_d = jnp.where(match[:, None, None], values[:, slot], a_d)
            covered = covered | match
        p_d = product[:, d * width:(d + 1) * width].reshape(row_blocks, width, width)
        r_d = jnp.where(covered[:, None, None], a_d.astype(jnp.float32) / p_d, 0.0)
        chunks.append(r_d.astype(jnp.bfloat16).reshape(tile_rows, width))
    ratios_rest = jnp.concatenate(chunks[1:], axis=1)
    numer_h_all = jnp.concatenate(
        [
            jnp.einsum("ik,ij->kj", w_tile, chunks[0], preferred_element_type=jnp.float32),
            jnp.einsum("ik,ij->kj", w_tile, ratios_rest, preferred_element_type=jnp.float32),
        ],
        axis=1,
    )
    numer_w = jnp.einsum(
        "ij,kj->ik", chunks[0], h_stack[0], preferred_element_type=jnp.float32
    ) + jnp.einsum("ij,kj->ik", ratios_rest, h_rest, preferred_element_type=jnp.float32)
    starts = [((-e) % n_row) * width for e in range(n_row)]
    return [numer_h_all[:, s:s + width] for s in starts], numer_w


def slot_terms(values, lists, counts, w_tile, h_stack, row_index):
    row_blocks, stored, width = values.shape[0], values.shape[1], values.shape[2]
    n_row, rank = h_stack.shape[0], h_stack.shape[1]
    tile_rows = w_tile.shape[0]
    w_rows = w_tile.reshape(row_blocks, width, rank)
    numer_h_stack = jnp.zeros((n_row, rank, width), jnp.float32)
    parts_w = []
    for brow in range(row_blocks):
        part_w = jnp.zeros((width, rank), jnp.float32)
        for slot in range(stored):
            target = lists[brow, slot]
            live = slot < counts[brow]
            h_block = lax.dynamic_index_in_dim(
                h_stack, (row_index - target) % n_row, 0, keepdims=False
            )
            product = jnp.dot(w_rows[brow], h_block, preferred_element_type=jnp.float32)
            ratios = (values[brow, slot].astype(jnp.float32) / product).astype(jnp.bfloat16)
            ratios = jnp.where(live, ratios, jnp.zeros_like(ratios))
            part_h = jnp.einsum(
                "ik,ij->kj", w_rows[brow], ratios, preferred_element_type=jnp.float32
            )
            part_w = part_w + jnp.einsum(
                "ij,kj->ik", ratios, h_block, preferred_element_type=jnp.float32
            )
            offset = (target - row_index) % n_row
            old = lax.dynamic_index_in_dim(numer_h_stack, offset, 0, keepdims=True)
            numer_h_stack = lax.dynamic_update_index_in_dim(
                numer_h_stack, old + part_h[None], offset, 0
            )
        parts_w.append(part_w)
    numer_w = jnp.stack(parts_w).reshape(tile_rows, rank)
    return [numer_h_stack[e] for e in range(n_row)], numer_w


def body(a_blocks, block_list, block_count, w_factor, h_factor):
    values = a_blocks[0, 0]
    lists = block_list[0, 0]
    counts = block_count[0, 0]
    w_tile = w_factor[0]
    row_blocks, stored, width = values.shape[0], values.shape[1], values.shape[2]
    rank = w_tile.shape[1]
    tile_rows = w_tile.shape[0]
    n_row = lax.axis_size("row")
    n_col = lax.axis_size("col")
    n_sub = lax.axis_size("sub")
    row_index = lax.axis_index("row")
    col_index = lax.axis_index("col")

    sub_index = lax.axis_index("sub")
    half = width // n_sub
    own_piece = h_factor[:, :half]
    for p in range(1, n_sub):
        own_piece = jnp.where(sub_index == p, h_factor[:, p * half:(p + 1) * half], own_piece)
    arrived = {d: shifted(own_piece, "row", d) for d in reversed(range(1, n_row))}
    fetched = jnp.stack([arrived[d] for d in range(1, n_row)])
    swapped = [fetched] + [shifted(fetched, "sub", k) for k in range(1, n_sub)]
    others = assemble(swapped, sub_index, n_sub, 2)
    h_stack = jnp.concatenate([h_factor[None], others])
    h_sum = jnp.sum(h_stack.astype(jnp.float32), axis=(0, 2))
    w_sum = jnp.sum(w_tile.astype(jnp.float32), axis=0)

    if tile_rows * n_row * width * 4 <= (8 << 20):
        numer_h_stack, numer_w = dense_terms(values, lists, counts, w_tile, h_stack, row_index)
    else:
        numer_h_stack, numer_w = slot_terms(values, lists, counts, w_tile, h_stack, row_index)

    share = tile_rows // n_col
    chunks = numer_w.reshape(n_col, share, rank)
    h_rows = as_rows(h_sum, rank)
    mine_w = lax.dynamic_index_in_dim(chunks, col_index, 0, keepdims=False)
    got_h = h_rows
    for d in range(1, n_col):
        chunk = lax.dynamic_index_in_dim(chunks, (col_index + d) % n_col, 0, keepdims=False)
        message = shifted(jnp.concatenate([chunk, h_rows]), "col", d)
        mine_w = mine_w + message[:share]
        got_h = got_h + message[share:]
    h_total = from_rows(got_h, rank)

    w_rows_sum = as_rows(w_sum, width)
    messages = [
        jnp.concatenate([x[:, p * half:(p + 1) * half] for x in numer_h_stack + [w_rows_sum]])
        for p in range(n_sub)
    ]
    def piece_message(k):
        want = (sub_index + k) % n_sub
        chosen = messages[0]
        for p in range(1, n_sub):
            chosen = jnp.where(want == p, messages[p], chosen)
        return chosen
    reduced = piece_message(0)
    for k in range(1, n_sub):
        reduced = reduced + shifted(piece_message(k), "sub", k)
    extra = reduced[n_row * rank:]
    mine_h = reduced[:rank]
    got_w = extra
    for d in reversed(range(1, n_row)):
        message = shifted(jnp.concatenate([reduced[d * rank:(d + 1) * rank], extra]), "row", d)
        mine_h = mine_h + message[:rank]
        got_w = got_w + message[rank:]
    final = jnp.concatenate([mine_h, got_w])
    total = assemble([final] + [shifted(final, "sub", k) for k in range(1, n_sub)], sub_index, n_sub, 1)
    numer_h = total[:rank]
    w_total = from_rows(total[rank:], rank)

    h_new = h_factor.astype(jnp.float32) * numer_h * (1.0 / w_total)[:, None]
    w_part = lax.dynamic_slice_in_dim(w_tile, col_index * share, share, 0).astype(jnp.float32)
    w_new = (w_part * mine_w * (1.0 / h_total)[None, :])[None]
    return (w_new, h_new)


def solution(mesh):
    placed = (
        P(("grp", "row", "sub"), "col", None, None, None, None),
        P(("grp", "row", "sub"), "col", None, None),
        P(("grp", "row", "sub"), "col", None),
        P(("grp", "row", "sub"), None, None),
        P(None, ("grp", "row", "col")),
    )
    return jax.shard_map(
        body,
        mesh=mesh,
        in_specs=placed,
        out_specs=(P(("grp", "row", "sub"), "col", None), P(None, ("grp", "row", "col"))),
        check_vma=False,
    )
```

```python
import jax
import jax.numpy as jnp
from jax import lax
from jax.sharding import PartitionSpec as P


def shifted(value, axis, by):
    length = lax.axis_size(axis)
    return lax.ppermute(value, axis, [(i, (i + by) % length) for i in range(length)])


def as_rows(vector, width):
    size = vector.shape[0]
    rows = -(-size // width)
    flat = jnp.pad(vector, (0, rows * width - size)).reshape(rows, width)
    return jnp.pad(flat, ((0, (-rows) % 8), (0, 0)))


def from_rows(rows, size):
    return rows.reshape(-1)[:size]


def assemble(pieces, index, count, axis):
    out = []
    for j in range(count):
        want = (index - j) % count
        chosen = pieces[0]
        for k in range(1, count):
            chosen = jnp.where(want == k, pieces[k], chosen)
        out.append(chosen)
    return jnp.concatenate(out, axis=axis)


def dense_terms(values, lists, counts, w_tile, h_stack, row_index):
    row_blocks, stored, width = values.shape[0], values.shape[1], values.shape[2]
    n_row, rank = h_stack.shape[0], h_stack.shape[1]
    tile_rows = w_tile.shape[0]
    h_rest = jnp.concatenate([h_stack[d] for d in range(1, n_row)], axis=1)
    product = jnp.concatenate(
        [
            jnp.dot(w_tile, h_stack[0], preferred_element_type=jnp.float32),
            jnp.dot(w_tile, h_rest, preferred_element_type=jnp.float32),
        ],
        axis=1,
    )
    chunks = []
    for d in range(n_row):
        block = (row_index - d) % n_row
        a_d = jnp.zeros((row_blocks, width, width), values.dtype)
        covered = jnp.zeros((row_blocks,), jnp.bool_)
        for slot in range(stored):
            match = (lists[:, slot] == block) & (slot < counts)
            a_d = jnp.where(match[:, None, None], values[:, slot], a_d)
            covered = covered | match
        p_d = product[:, d * width:(d + 1) * width].reshape(row_blocks, width, width)
        r_d = jnp.where(covered[:, None, None], a_d.astype(jnp.float32) / p_d, 0.0)
        chunks.append(r_d.astype(jnp.bfloat16).reshape(tile_rows, width))
    ratios_rest = jnp.concatenate(chunks[1:], axis=1)
    numer_h_all = jnp.concatenate(
        [
            jnp.einsum("ik,ij->kj", w_tile, chunks[0], preferred_element_type=jnp.float32),
            jnp.einsum("ik,ij->kj", w_tile, ratios_rest, preferred_element_type=jnp.float32),
        ],
        axis=1,
    )
    numer_w = jnp.einsum(
        "ij,kj->ik", chunks[0], h_stack[0], preferred_element_type=jnp.float32
    ) + jnp.einsum("ij,kj->ik", ratios_rest, h_rest, preferred_element_type=jnp.float32)
    starts = [((-e) % n_row) * width for e in range(n_row)]
    return [numer_h_all[:, s:s + width] for s in starts], numer_w


def slot_terms(values, lists, counts, w_tile, h_stack, row_index):
    row_blocks, stored, width = values.shape[0], values.shape[1], values.shape[2]
    n_row, rank = h_stack.shape[0], h_stack.shape[1]
    tile_rows = w_tile.shape[0]
    w_rows = w_tile.reshape(row_blocks, width, rank)
    numer_h_stack = jnp.zeros((n_row, rank, width), jnp.float32)
    parts_w = []
    for brow in range(row_blocks):
        part_w = jnp.zeros((width, rank), jnp.float32)
        for slot in range(stored):
            target = lists[brow, slot]
            live = slot < counts[brow]
            h_block = lax.dynamic_index_in_dim(
                h_stack, (row_index - target) % n_row, 0, keepdims=False
            )
            product = jnp.dot(w_rows[brow], h_block, preferred_element_type=jnp.float32)
            ratios = (values[brow, slot].astype(jnp.float32) / product).astype(jnp.bfloat16)
            ratios = jnp.where(live, ratios, jnp.zeros_like(ratios))
            part_h = jnp.einsum(
                "ik,ij->kj", w_rows[brow], ratios, preferred_element_type=jnp.float32
            )
            part_w = part_w + jnp.einsum(
                "ij,kj->ik", ratios, h_block, preferred_element_type=jnp.float32
            )
            offset = (target - row_index) % n_row
            old = lax.dynamic_index_in_dim(numer_h_stack, offset, 0, keepdims=True)
            numer_h_stack = lax.dynamic_update_index_in_dim(
                numer_h_stack, old + part_h[None], offset, 0
            )
        parts_w.append(part_w)
    numer_w = jnp.stack(parts_w).reshape(tile_rows, rank)
    return [numer_h_stack[e] for e in range(n_row)], numer_w


def pair_exchange(numer_h_stack, w_rows_sum, sub_index, rank, half):
    n_row = len(numer_h_stack)

    def halves(x):
        lo, hi = x[:, :half], x[:, half:]
        return jnp.where(sub_index == 0, lo, hi), jnp.where(sub_index == 0, hi, lo)

    kept, sent = zip(*[halves(x) for x in numer_h_stack[1:] + [w_rows_sum]])
    reduced = jnp.concatenate(kept) + shifted(jnp.concatenate(sent), "sub", 1)
    extra = reduced[(n_row - 1) * rank:]
    own_mine, own_theirs = halves(numer_h_stack[0])
    mine_h = own_mine
    got_w = extra
    for d in reversed(range(1, n_row)):
        message = jnp.concatenate([reduced[(d - 1) * rank:d * rank], extra])
        message = shifted(message, "row", d)
        mine_h = mine_h + message[:rank]
        got_w = got_w + message[rank:]
    final = jnp.concatenate([mine_h, got_w])
    got = shifted(jnp.concatenate([final, own_theirs]), "sub", 1)
    extra_rows = final.shape[0] - rank
    mine = jnp.concatenate([final[:rank] + got[final.shape[0]:], final[rank:]])
    theirs = jnp.concatenate([got[:rank] + own_theirs, got[rank:final.shape[0]]])
    total = assemble([mine, theirs], sub_index, 2, 1)
    return total[:rank], from_rows(total[rank:rank + extra_rows], rank)


def body(a_blocks, block_list, block_count, w_factor, h_factor):
    values = a_blocks[0, 0]
    lists = block_list[0, 0]
    counts = block_count[0, 0]
    w_tile = w_factor[0]
    row_blocks, stored, width = values.shape[0], values.shape[1], values.shape[2]
    rank = w_tile.shape[1]
    tile_rows = w_tile.shape[0]
    n_row = lax.axis_size("row")
    n_col = lax.axis_size("col")
    n_sub = lax.axis_size("sub")
    row_index = lax.axis_index("row")
    col_index = lax.axis_index("col")

    sub_index = lax.axis_index("sub")
    half = width // n_sub
    own_piece = h_factor[:, :half]
    for p in range(1, n_sub):
        own_piece = jnp.where(sub_index == p, h_factor[:, p * half:(p + 1) * half], own_piece)
    arrived = {d: shifted(own_piece, "row", d) for d in reversed(range(1, n_row))}
    fetched = jnp.stack([arrived[d] for d in range(1, n_row)])
    swapped = [fetched] + [shifted(fetched, "sub", k) for k in range(1, n_sub)]
    others = assemble(swapped, sub_index, n_sub, 2)
    h_stack = jnp.concatenate([h_factor[None], others])
    h_sum = jnp.sum(h_stack.astype(jnp.float32), axis=(0, 2))
    w_sum = jnp.sum(w_tile.astype(jnp.float32), axis=0)

    if tile_rows * n_row * width * 4 <= (8 << 20):
        numer_h_stack, numer_w = dense_terms(values, lists, counts, w_tile, h_stack, row_index)
    else:
        numer_h_stack, numer_w = slot_terms(values, lists, counts, w_tile, h_stack, row_index)

    share = tile_rows // n_col
    chunks = numer_w.reshape(n_col, share, rank)
    h_rows = as_rows(h_sum, rank)
    mine_w = lax.dynamic_index_in_dim(chunks, col_index, 0, keepdims=False)
    got_h = h_rows
    for d in range(1, n_col):
        chunk = lax.dynamic_index_in_dim(chunks, (col_index + d) % n_col, 0, keepdims=False)
        message = shifted(jnp.concatenate([chunk, h_rows]), "col", d)
        mine_w = mine_w + message[:share]
        got_h = got_h + message[share:]
    h_total = from_rows(got_h, rank)

    w_rows_sum = as_rows(w_sum, width)
    if n_sub == 2:
        numer_h, w_total = pair_exchange(numer_h_stack, w_rows_sum, sub_index, rank, half)
    else:
        messages = [
            jnp.concatenate([x[:, p * half:(p + 1) * half] for x in numer_h_stack + [w_rows_sum]])
            for p in range(n_sub)
        ]
        def piece_message(k):
            want = (sub_index + k) % n_sub
            chosen = messages[0]
            for p in range(1, n_sub):
                chosen = jnp.where(want == p, messages[p], chosen)
            return chosen
        reduced = piece_message(0)
        for k in range(1, n_sub):
            reduced = reduced + shifted(piece_message(k), "sub", k)
        extra = reduced[n_row * rank:]
        mine_h = reduced[:rank]
        got_w = extra
        for d in reversed(range(1, n_row)):
            message = shifted(jnp.concatenate([reduced[d * rank:(d + 1) * rank], extra]), "row", d)
            mine_h = mine_h + message[:rank]
            got_w = got_w + message[rank:]
        final = jnp.concatenate([mine_h, got_w])
        total = assemble([final] + [shifted(final, "sub", k) for k in range(1, n_sub)], sub_index, n_sub, 1)
        numer_h = total[:rank]
        w_total = from_rows(total[rank:], rank)


    h_new = h_factor.astype(jnp.float32) * numer_h / w_total[:, None]
    w_part = lax.dynamic_slice_in_dim(w_tile, col_index * share, share, 0).astype(jnp.float32)
    w_new = (w_part * mine_w / h_total[None, :])[None]
    return (w_new, h_new)


def solution(mesh):
    placed = (
        P(("grp", "row", "sub"), "col", None, None, None, None),
        P(("grp", "row", "sub"), "col", None, None),
        P(("grp", "row", "sub"), "col", None),
        P(("grp", "row", "sub"), None, None),
        P(None, ("grp", "row", "col")),
    )
    return jax.shard_map(
        body,
        mesh=mesh,
        in_specs=placed,
        out_specs=(P(("grp", "row", "sub"), "col", None), P(None, ("grp", "row", "col"))),
        check_vma=False,
    )
```
